512 devices in a mesh: dp: 64 (over z, y), tensor: 4 (over x), sect: 2 (over core).
Axes of the slice: x: 4, y: 8, z: 8, core: 2. Of those that a mesh axis runs over, the one named last changes fastest.
Arguments:
- tokens: bfloat16 [4096, 2048], P(('dp', 'sect'), 'tensor'), may hold values from -6 to 6
- route_experts: int32 [4096, 8], P(('dp', 'sect')), may hold values from 0 to 127, all different within a row; in each aligned block of 32 rows (0 to 31, 32 to 63, ...) at most 5 rows name the same one
- route_weights: float32 [4096, 8], P(('dp', 'sect')), may hold values from 0.05 to 1
- gate_weight: bfloat16 [128, 2048, 768], P(('dp', 'sect'), None, 'tensor'), may hold values from -0.125 to 0.125
- up_weight: bfloat16 [128, 2048, 768], P(('dp', 'sect'), None, 'tensor'), may hold values from -0.125 to 0.125
- down_weight: bfloat16 [128, 768, 2048], P(('dp', 'sect'), 'tensor'), may hold values from -0.21875 to 0.21875
- query: bfloat16 [4096, 64, 128], P(('dp', 'sect'), 'tensor'), may hold values from -48 to 48
- cache_keys: bfloat16 [4096, 128, 4, 128], P(('dp', 'sect'), None, 'tensor'), may hold values from -16 to 16
- cache_values: bfloat16 [4096, 128, 4, 128], P(('dp', 'sect'), None, 'tensor'), may hold values from -6 to 6
- lengths: int32 [4096], P(('dp', 'sect')), may hold values from 2 to 128, as said below
Outputs:
- mixture: bfloat16 [4096, 2048], P(('dp', 'sect'), 'tensor')
- attention: bfloat16 [4096, 64, 128], P(('dp', 'sect'), 'tensor')
The draws below stay inside these ranges and needn't reach their ends.
Inputs may be any that keep to these rules, and one draw needn't show every extreme that they name: `route_experts`: each row names 8 different experts; in each block of 32 rows no expert is named more than 5 times, a bound that some block reaches. `lengths`: every block's first row has all 128 positions filled.
All inputs are finite; a program needn't handle non-finite values.
Results may differ from the reference program's by a relative error of at most 0.015.
Values may be sent and summed in bfloat16 or wider, within the bound.
No kernel may reach another device: no remote copies, remote signals or barrier semaphores. Data moves between devices by JAX's collectives and lax.ppermute only.
A program may use at most 64 MiB of HBM per device.

```python
import math
import jax
import jax.numpy as jnp
import numpy as np
from jax import lax

D = 2048
FFW = 768
EXPERTS = 128
TOP = 8
QH = 64
KVH = 4
HD = 128
CAP = 5
LEN = 128
ROW_DEV = 32
ROWS = 4096
N_TENSOR = 4


def drawn_parts(key):
    normal_keys = jnp.clip(jax.random.normal(jax.random.fold_in(key, 101), (ROWS, LEN, KVH, HD), jnp.float32), -5.0, 5.0)
    return normal_keys


def draw_cache_keys(key, part):
    normal_keys = drawn_parts(key)
    return normal_keys.astype(jnp.bfloat16)


def draw_query(key, part):
    drawn = jnp.clip(jax.random.normal(jax.random.fold_in(key, 104), (ROWS, QH, HD), jnp.float32), -5.0, 5.0)
    return drawn.astype(jnp.bfloat16)


def draw_lengths(key, part):
    drawn = jax.random.randint(jax.random.fold_in(key, 105), (ROWS,), 2, LEN + 1, dtype=jnp.int32)
    ordinal = jnp.arange(ROWS, dtype=jnp.int32)
    return jnp.where(ordinal % ROW_DEV == 0, LEN, drawn).astype(jnp.int32)


def block_scale(rng, dims, pieces, least, high):
    def one(dim, parts):
        draws = jax.random.uniform(jax.random.fold_in(jax.random.fold_in(rng, 6), dim), (parts,), jnp.float32, least / len(pieces), high / len(pieces))
        return jnp.repeat(jnp.exp(draws), dims[dim] // parts).reshape((-1,) + (1,) * (len(dims) - dim - 1))

    level = one(*pieces[0])
    for cut in pieces[1:]:
        level = level * one(*cut)
    return level


def routed_block(own_key, own, number, rows, number_of, top, bound, skew):
    order = jax.random.permutation(own_key, number_of)
    crowded, common = shares(number_of, rows * top, bound, skew, True), shares(number_of, rows * top, bound, skew, False)
    places = jnp.arange(number_of)

    def named(sizes, offset_by):
        used = int((sizes > 0).sum())
        fixed = max(1, used // 4)
        passed = fixed + (places - fixed + offset_by * (used - fixed)) % max(1, number_of - fixed)
        return jnp.zeros((number_of,), jnp.int32).at[order[jnp.where(places < fixed, places, passed)]].set(jnp.asarray(sizes, jnp.int32))

    sizes = jnp.where(number % 4 == 0, named(crowded, number // 4), named(common, number - number // 4 - 1))
    mixed = jax.random.permutation(jax.random.fold_in(own, 3), number_of)
    source_of, receiver = mixed[0:number_of // 2 * 2:2], mixed[1:number_of // 2 * 2:2]
    margin = jnp.minimum(sizes[source_of] - 1, bound - sizes[receiver]) // 2
    margin = jnp.where((source_of == order[0]) | (receiver == order[0]) | (sizes[receiver] == 0), 0, jnp.maximum(margin, 0))
    passed = jax.random.randint(jax.random.fold_in(own, 4), (number_of // 2,), 0, 1 << 20) % (margin + 1)
    sizes = sizes.at[source_of].add(-passed).at[receiver].add(passed)
    items = jnp.searchsorted(jnp.cumsum(sizes), jnp.arange(rows * top), side="right").astype(jnp.int32)
    listing = items.reshape(top, rows).T
    listing = listing[jax.random.permutation(jax.random.fold_in(own, 1), rows)]
    offset_by = jax.random.randint(jax.random.fold_in(own, 2), (rows, 1), 0, top)
    return jnp.take_along_axis(listing, (jnp.arange(top)[None, :] + offset_by) % top, axis=1)


def shares(count, total, reach, slope, full):
    portions = [(1 << 20) // math.isqrt(rank ** slope) + 1 for rank in range(1, count + 1)]
    largest = reach if full else min(reach, max(-(-total // count), total * portions[0] // sum(portions)))
    least = 1 if total - largest >= count - 1 else 0
    given, rest = [largest] + [least] * (count - 1), total - largest - least * (count - 1)
    while rest > 0:
        free = [i for i in range(1, count) if given[i] < largest] or [i for i in range(1, count) if given[i] < reach]
        whole, budget = sum([portions[i] for i in free]), rest
        for i in free:
            extra = min(reach - given[i], max(1, budget * portions[i] // whole), rest)
            given[i] = given[i] + extra
            rest = rest - extra
    return np.array(given)


def scatter_about(stream_key, shape, scale, bound, cuts=(), kind=jnp.bfloat16):
    values = jax.random.normal(stream_key, shape, jnp.float32) * scale
    if len(cuts) > 0:
        values = block_scale(stream_key, shape, cuts, -0.22, 0.18) * values
    return jnp.clip(values, min=-bound, max=bound).astype(kind)


def setup_inputs(seed: int = 0) -> dict:
    key_of = jax.random.split(jax.random.key(seed), 11)
    tokens = scatter_about(key_of[0], (ROWS, D), 1.0, 6.0, ((0, 128), (1, 4)))
    route_experts_keys = jax.random.split(jax.random.fold_in(key_of[1], 1), ROWS // ROW_DEV)
    route_experts_turns = jax.random.permutation(jax.random.fold_in(key_of[1], 3), ROWS // ROW_DEV)
    route_experts = jax.vmap(lambda own, number: routed_block(jax.random.fold_in(key_of[1], 2), own, number, ROW_DEV, EXPERTS, TOP, CAP, 2))(route_experts_keys, route_experts_turns).reshape((ROWS, TOP))
    route_weights = jnp.clip(jnp.exp(math.log(1.0) - 2.9957323 * jax.random.uniform(key_of[2], (ROWS, TOP), jnp.float32) ** block_scale(key_of[2], (ROWS, TOP), ((0, 128),), -0.2, 0.2)), 0.05, 1.0)
    gate_weight = scatter_about(key_of[3], (EXPERTS, D, FFW), D ** -0.5, 0.125, ((0, 128), (2, 4)))
    up_weight = scatter_about(key_of[4], (EXPERTS, D, FFW), D ** -0.5, 0.125, ((0, 128), (2, 4)))
    down_weight = scatter_about(key_of[5], (EXPERTS, FFW, D), FFW ** -0.5, 0.21875, ((0, 128), (1, 4)))
    query = draw_query(jax.random.fold_in(key_of[10], 71), 0)
    cache_keys = draw_cache_keys(jax.random.fold_in(key_of[10], 71), 0)
    cache_values = scatter_about(key_of[8], (ROWS, LEN, KVH, HD), 1.0, 6.0, ((0, 128), (2, 4)))
    lengths = draw_lengths(jax.random.fold_in(key_of[10], 71), 0)
    return {"tokens": tokens, "route_experts": route_experts, "route_weights": route_weights, "gate_weight": gate_weight, "up_weight": up_weight, "down_weight": down_weight, "query": query, "cache_keys": cache_keys, "cache_values": cache_values, "lengths": lengths}


def route_tables(expert_ids, weights, experts, capacity):
    row_count, top_count = expert_ids.shape
    pair_count = row_count * top_count
    flat_ids = expert_ids.reshape(pair_count).astype(jnp.int32)
    one_hot = (flat_ids[:, None] == jnp.arange(experts, dtype=jnp.int32)[None, :]).astype(jnp.float32)
    ordinal = jnp.arange(pair_count, dtype=jnp.int32)
    earlier = (ordinal[:, None] > ordinal[None, :]).astype(jnp.float32)
    counts = jnp.dot(earlier, one_hot, preferred_element_type=jnp.float32)
    slot_index = jnp.sum(counts * one_hot, axis=1).astype(jnp.int32)
    target = flat_ids * capacity + slot_index
    select = (jnp.arange(experts * capacity, dtype=jnp.int32)[:, None] == target[None, :]).astype(jnp.float32)
    select = select.reshape(experts * capacity, row_count, top_count)
    share_norm = (weights / jnp.sum(weights, axis=1, keepdims=True)).astype(jnp.bfloat16)
    share_norm = lax.optimization_barrier(share_norm).astype(jnp.float32)
    dispatch = jnp.sum(select, axis=2).astype(jnp.bfloat16)
    combine = jnp.sum(select * share_norm[None, :, :], axis=2).astype(jnp.bfloat16)
    return dispatch, combine


def expert_block(inputs, w_gate, w_up, w_down):
    gate_part = jnp.dot(inputs, w_gate, preferred_element_type=jnp.float32)
    up_part = jnp.dot(inputs, w_up, preferred_element_type=jnp.float32)
    hidden = (jax.nn.silu(gate_part) * up_part).astype(jnp.bfloat16)
    width = hidden.shape[1] // N_TENSOR
    total = jnp.zeros((inputs.shape[0], w_down.shape[1]), jnp.float32)
    for group in range(N_TENSOR):
        partial_sum = jnp.dot(hidden[:, group * width:(group + 1) * width], w_down[group * width:(group + 1) * width], preferred_element_type=jnp.float32)
        rounded = lax.optimization_barrier(partial_sum.astype(jnp.bfloat16))
        total = total + rounded.astype(jnp.float32)
    return total.astype(jnp.bfloat16)


def reference(tokens, route_experts, route_weights, gate_weight, up_weight, down_weight, query, cache_keys, cache_values, lengths):
    block_count = ROWS // ROW_DEV
    dispatch, combine = jax.vmap(lambda ids_part, weight_part: route_tables(ids_part, weight_part, EXPERTS, CAP))(
        route_experts.reshape(block_count, ROW_DEV, TOP), route_weights.reshape(block_count, ROW_DEV, TOP))
    token_blocks = tokens.reshape(block_count, ROW_DEV, D)
    buffers = lax.map(lambda items: jnp.dot(items[0], items[1], preferred_element_type=jnp.float32).astype(jnp.bfloat16), (dispatch, token_blocks))
    per_expert = buffers.reshape(block_count, EXPERTS, CAP, D).transpose(1, 0, 2, 3).reshape(EXPERTS, block_count * CAP, D)
    outputs = lax.map(lambda items: expert_block(items[0], items[1], items[2], items[3]), (per_expert, gate_weight, up_weight, down_weight))
    returned = outputs.reshape(EXPERTS, block_count, CAP, D).transpose(1, 0, 2, 3).reshape(block_count, EXPERTS * CAP, D)
    mixture = lax.map(lambda items: jnp.dot(items[0].T, items[1], preferred_element_type=jnp.float32).astype(jnp.bfloat16), (combine, returned))
    mixture = mixture.reshape(ROWS, D)

    group_size = QH // KVH
    queries = query.astype(jnp.float32).reshape(ROWS, KVH, group_size, HD)
    scores = jnp.einsum("rkgd,rlkd->rkgl", queries, cache_keys.astype(jnp.float32)) * (HD ** -0.5)
    valid = jnp.arange(LEN, dtype=jnp.int32)[None, :] < lengths[:, None]
    scores = jnp.where(valid[:, None, None, :], scores, -1e30)
    highest = jnp.max(scores, axis=3, keepdims=True)
    expo = jnp.exp(scores - highest)
    probs = (expo / jnp.sum(expo, axis=3, keepdims=True)).astype(jnp.bfloat16)
    attention = jnp.einsum("rkgl,rlkd->rkgd", probs.astype(jnp.float32), cache_values.astype(jnp.float32))
    attention = attention.astype(jnp.bfloat16).reshape(ROWS, QH, HD)
    return mixture, attention
```

```python
import jax
import jax.numpy as jnp
from jax import lax
from jax.sharding import PartitionSpec as P

EXPERTS = 128
CAP = 5


def route_tables(expert_ids, weights, experts, capacity):
    row_count, top_count = expert_ids.shape
    pair_count = row_count * top_count
    flat_ids = expert_ids.reshape(pair_count)
    one_hot = (flat_ids[:, None] == jnp.arange(experts, dtype=jnp.int32)[None, :]).astype(
        jnp.float32
    )
    ordinal = jnp.arange(pair_count, dtype=jnp.int32)
    earlier = (ordinal[:, None] > ordinal[None, :]).astype(jnp.float32)
    counts = jnp.dot(earlier, one_hot, preferred_element_type=jnp.float32)
    slot_index = jnp.sum(counts * one_hot, axis=1).astype(jnp.int32)
    target = flat_ids * capacity + slot_index
    select = (jnp.arange(experts * capacity, dtype=jnp.int32)[:, None] == target[None, :]).astype(
        jnp.float32
    )
    select = select.reshape(experts * capacity, row_count, top_count)
    share_norm = (weights / jnp.sum(weights, axis=1, keepdims=True)).astype(jnp.bfloat16)
    share_norm = lax.optimization_barrier(share_norm).astype(jnp.float32)
    dispatch = jnp.sum(select, axis=2).astype(jnp.bfloat16)
    combine = jnp.sum(select * share_norm[None, :, :], axis=2).astype(jnp.bfloat16)
    return (dispatch, combine)


def attend(query, cache_keys, cache_values, lengths):
    row_count, head_count, head_size = query.shape
    kv_count = cache_keys.shape[2]
    group_size = head_count // kv_count
    queries = query.reshape(row_count, kv_count, group_size, head_size)
    scores = jnp.einsum(
        "rkgd,rlkd->rkgl", queries, cache_keys, preferred_element_type=jnp.float32
    ) * head_size ** (-0.5)
    valid = jnp.arange(cache_keys.shape[1], dtype=jnp.int32)[None, :] < lengths[:, None]
    scores = jnp.where(valid[:, None, None, :], scores, -1e30)
    highest = jnp.max(scores, axis=3, keepdims=True)
    expo = jnp.exp(scores - highest)
    probs = (expo / jnp.sum(expo, axis=3, keepdims=True)).astype(jnp.bfloat16)
    result = jnp.einsum("rkgl,rlkd->rkgd", probs, cache_values, preferred_element_type=jnp.float32)
    return result.astype(jnp.bfloat16).reshape(row_count, head_count, head_size)


def local(
    tokens,
    route_experts,
    route_weights,
    gate_weight,
    up_weight,
    down_weight,
    query,
    cache_keys,
    cache_values,
    lengths,
):
    owners = lax.axis_size("dp") * lax.axis_size("sect")
    dispatch, combine = route_tables(route_experts, route_weights, EXPERTS, CAP)
    slot_total = EXPERTS * CAP
    per_owner = slot_total // owners
    local_buffer = jnp.dot(dispatch, tokens, preferred_element_type=jnp.float32).astype(
        jnp.bfloat16
    )
    local_buffer = local_buffer.reshape(owners, per_owner, local_buffer.shape[1])
    arrived = lax.all_to_all(local_buffer, ("dp", "sect"), split_axis=0, concat_axis=0, tiled=True)
    own_experts = gate_weight.shape[0]
    width = arrived.shape[2]
    pieces = lax.axis_size("tensor")
    inputs = (
        arrived.reshape(owners, own_experts, CAP, width)
        .transpose(1, 0, 2, 3)
        .reshape(own_experts, owners * CAP, width)
    )
    gathered = lax.all_gather(inputs, "tensor", axis=0, tiled=False)
    hidden_width = gate_weight.shape[2]
    gate_view = gate_weight.reshape(own_experts, pieces, width, hidden_width)
    up_view = up_weight.reshape(own_experts, pieces, width, hidden_width)
    gate_part = jnp.einsum(
        "tend,etdf->enf", gathered, gate_view, preferred_element_type=jnp.float32
    )
    up_part = jnp.einsum("tend,etdf->enf", gathered, up_view, preferred_element_type=jnp.float32)
    hidden = (jax.nn.silu(gate_part) * up_part).astype(jnp.bfloat16)
    partial_sum = jnp.einsum(
        "enf,efd->end", hidden, down_weight, preferred_element_type=jnp.float32
    )
    summed = lax.psum_scatter(
        partial_sum.astype(jnp.bfloat16), "tensor", scatter_dimension=2, tiled=True
    )
    last = summed.shape[2]
    returned = lax.all_to_all(
        summed.reshape(own_experts, owners, CAP, last)
        .transpose(1, 0, 2, 3)
        .reshape(owners, own_experts * CAP, last),
        ("dp", "sect"),
        split_axis=0,
        concat_axis=0,
        tiled=True,
    )
    expert_out = returned.reshape(slot_total, returned.shape[2])
    mixture = jnp.dot(combine.T, expert_out, preferred_element_type=jnp.float32).astype(
        jnp.bfloat16
    )
    attention = attend(query, cache_keys, cache_values, lengths)
    return (mixture, attention)


def solution(mesh):
    placed = (
        P(("dp", "sect"), "tensor"),
        P(("dp", "sect"), None),
        P(("dp", "sect"), None),
        P(("dp", "sect"), None, "tensor"),
        P(("dp", "sect"), None, "tensor"),
        P(("dp", "sect"), "tensor", None),
        P(("dp", "sect"), "tensor", None),
        P(("dp", "sect"), None, "tensor", None),
        P(("dp", "sect"), None, "tensor", None),
        P(("dp", "sect")),
    )
    return jax.shard_map(
        local,
        mesh=mesh,
        in_specs=placed,
        out_specs=(P(("dp", "sect"), "tensor"), P(("dp", "sect"), "tensor", None)),
        check_vma=False,
    )
```

```python
import jax
import jax.numpy as jnp
from jax import lax
from jax.sharding import PartitionSpec as P

EXPERTS = 128
CAP = 5


def route_tables(expert_ids, weights, experts, capacity):
    row_count, top_count = expert_ids.shape
    pair_count = row_count * top_count
    flat_ids = expert_ids.reshape(pair_count)
    one_hot = (flat_ids[:, None] == jnp.arange(experts, dtype=jnp.int32)[None, :]).astype(
        jnp.float32
    )
    ordinal = jnp.arange(pair_count, dtype=jnp.int32)
    earlier = (ordinal[:, None] > ordinal[None, :]).astype(jnp.float32)
    counts = jnp.dot(earlier, one_hot, preferred_element_type=jnp.float32)
    slot_index = jnp.sum(counts * one_hot, axis=1).astype(jnp.int32)
    target = flat_ids * capacity + slot_index
    select = (jnp.arange(experts * capacity, dtype=jnp.int32)[:, None] == target[None, :]).astype(
        jnp.float32
    )
    select = select.reshape(experts * capacity, row_count, top_count)
    share_norm = (weights / jnp.sum(weights, axis=1, keepdims=True)).astype(jnp.bfloat16)
    share_norm = lax.optimization_barrier(share_norm).astype(jnp.float32)
    dispatch = jnp.sum(select, axis=2).astype(jnp.bfloat16)
    combine = jnp.sum(select * share_norm[None, :, :], axis=2).astype(jnp.bfloat16)
    return (dispatch, combine)


def attend(query, cache_keys, cache_values, lengths):
    row_count, head_count, head_size = query.shape
    kv_count = cache_keys.shape[2]
    group_size = head_count // kv_count
    queries = query.reshape(row_count, kv_count, group_size, head_size)
    scores = jnp.einsum(
        "rkgd,rlkd->rkgl", queries, cache_keys, preferred_element_type=jnp.float32
    ) * head_size ** (-0.5)
    valid = jnp.arange(cache_keys.shape[1], dtype=jnp.int32)[None, :] < lengths[:, None]
    scores = jnp.where(valid[:, None, None, :], scores, -1e30)
    highest = jnp.max(scores, axis=3, keepdims=True)
    expo = jnp.exp(scores - highest)
    probs = (expo / jnp.sum(expo, axis=3, keepdims=True)).astype(jnp.bfloat16)
    result = jnp.einsum("rkgl,rlkd->rkgd", probs, cache_values, preferred_element_type=jnp.float32)
    return result.astype(jnp.bfloat16).reshape(row_count, head_count, head_size)


def local(
    tokens,
    route_experts,
    route_weights,
    gate_weight,
    up_weight,
    down_weight,
    query,
    cache_keys,
    cache_values,
    lengths,
):
    owners = lax.axis_size("dp") * lax.axis_size("sect")
    dispatch, combine = route_tables(route_experts, route_weights, EXPERTS, CAP)
    slot_total = EXPERTS * CAP
    per_owner = slot_total // owners
    local_buffer = jnp.dot(dispatch, tokens, preferred_element_type=jnp.float32).astype(
        jnp.bfloat16
    )
    local_buffer = local_buffer.reshape(owners, per_owner, local_buffer.shape[1])
    arrived = lax.all_to_all(local_buffer, ("dp", "sect"), split_axis=0, concat_axis=0, tiled=True)
    own_experts = gate_weight.shape[0]
    width = arrived.shape[2]
    pieces = lax.axis_size("tensor")
    inputs = (
        arrived.reshape(owners, own_experts, CAP, width)
        .transpose(1, 0, 2, 3)
        .reshape(own_experts, owners * CAP, width)
    )
    gathered = lax.all_gather(inputs, "tensor", axis=0, tiled=False)
    hidden_width = gate_weight.shape[2]
    gate_view = gate_weight.reshape(own_experts, pieces, width, hidden_width)
    up_view = up_weight.reshape(own_experts, pieces, width, hidden_width)
    gate_part = jnp.einsum(
        "tend,etdf->enf", gathered, gate_view, preferred_element_type=jnp.float32
    )
    up_part = jnp.einsum("tend,etdf->enf", gathered, up_view, preferred_element_type=jnp.float32)
    hidden = (jax.nn.silu(gate_part) * up_part).astype(jnp.bfloat16)
    out_width = down_weight.shape[2] // pieces
    down_mine = lax.all_to_all(
        down_weight.reshape(own_experts, hidden_width, pieces, out_width).transpose(2, 0, 1, 3),
        "tensor",
        split_axis=0,
        concat_axis=0,
        tiled=True,
    )
    hidden_all = lax.all_gather(hidden.transpose(0, 2, 1), "tensor", axis=0, tiled=False)
    group_sums = jnp.einsum(
        "gefn,gefc->genc", hidden_all, down_mine, preferred_element_type=jnp.float32
    ).astype(jnp.bfloat16)
    summed = jnp.sum(group_sums.astype(jnp.float32), axis=0).astype(jnp.bfloat16)
    last = summed.shape[2]
    returned = lax.all_to_all(
        summed.reshape(own_experts, owners, CAP, last)
        .transpose(1, 0, 2, 3)
        .reshape(owners, own_experts * CAP, last),
        ("dp", "sect"),
        split_axis=0,
        concat_axis=0,
        tiled=True,
    )
    expert_out = returned.reshape(slot_total, returned.shape[2])
    mixture = jnp.dot(combine.T, expert_out, preferred_element_type=jnp.float32).astype(
        jnp.bfloat16
    )
    attention = attend(query, cache_keys, cache_values, lengths)
    return (mixture, attention)


def solution(mesh):
    placed = (
        P(("dp", "sect"), "tensor"),
        P(("dp", "sect"), None),
        P(("dp", "sect"), None),
        P(("dp", "sect"), None, "tensor"),
        P(("dp", "sect"), None, "tensor"),
        P(("dp", "sect"), "tensor", None),
        P(("dp", "sect"), "tensor", None),
        P(("dp", "sect"), None, "tensor", None),
        P(("dp", "sect"), None, "tensor", None),
        P(("dp", "sect")),
    )
    return jax.shard_map(
        local,
        mesh=mesh,
        in_specs=placed,
        out_specs=(P(("dp", "sect"), "tensor"), P(("dp", "sect"), "tensor", None)),
        check_vma=False,
    )
```

```python
import jax
import jax.numpy as jnp
from jax import lax
from jax.sharding import PartitionSpec as P

EXPERTS = 128
CAP = 5


def route_tables(expert_ids, weights, experts, capacity):
    row_count, top_count = expert_ids.shape
    pair_count = row_count * top_count
    flat_ids = expert_ids.reshape(pair_count)
    one_hot = (flat_ids[:, None] == jnp.arange(experts, dtype=jnp.int32)[None, :]).astype(
        jnp.float32
    )
    ordinal = jnp.arange(pair_count, dtype=jnp.int32)
    earlier = (ordinal[:, None] > ordinal[None, :]).astype(jnp.float32)
    counts = jnp.dot(earlier, one_hot, preferred_element_type=jnp.float32)
    slot_index = jnp.sum(counts * one_hot, axis=1).astype(jnp.int32)
    target = flat_ids * capacity + slot_index
    select = (jnp.arange(experts * capacity, dtype=jnp.int32)[:, None] == target[None, :]).astype(
        jnp.float32
    )
    select = select.reshape(experts * capacity, row_count, top_count)
    share_norm = (weights / jnp.sum(weights, axis=1, keepdims=True)).astype(jnp.bfloat16)
    share_norm = lax.optimization_barrier(share_norm).astype(jnp.float32)
    dispatch = jnp.sum(select, axis=2).astype(jnp.bfloat16)
    combine = jnp.sum(select * share_norm[None, :, :], axis=2).astype(jnp.bfloat16)
    return (dispatch, combine)


def attend(query, cache_keys, cache_values, lengths):
    row_count, head_count, head_size = query.shape
    kv_count = cache_keys.shape[2]
    group_size = head_count // kv_count
    queries = query.reshape(row_count, kv_count, group_size, head_size)
    scores = jnp.einsum(
        "rkgd,rlkd->rkgl", queries, cache_keys, preferred_element_type=jnp.float32
    ) * head_size ** (-0.5)
    valid = jnp.arange(cache_keys.shape[1], dtype=jnp.int32)[None, :] < lengths[:, None]
    scores = jnp.where(valid[:, None, None, :], scores, -1e30)
    highest = jnp.max(scores, axis=3, keepdims=True)
    expo = jnp.exp(scores - highest)
    probs = (expo / jnp.sum(expo, axis=3, keepdims=True)).astype(jnp.bfloat16)
    result = jnp.einsum("rkgl,rlkd->rkgd", probs, cache_values, preferred_element_type=jnp.float32)
    return result.astype(jnp.bfloat16).reshape(row_count, head_count, head_size)


def local(
    tokens,
    route_experts,
    route_weights,
    gate_weight,
    up_weight,
    down_weight,
    query,
    cache_keys,
    cache_values,
    lengths,
):
    owners = lax.axis_size("dp") * lax.axis_size("sect")
    dispatch, combine = route_tables(route_experts, route_weights, EXPERTS, CAP)
    slot_total = EXPERTS * CAP
    per_owner = slot_total // owners
    local_buffer = jnp.dot(dispatch, tokens, preferred_element_type=jnp.float32).astype(
        jnp.bfloat16
    )
    width = local_buffer.shape[1]
    lanes = 128
    local_buffer = local_buffer.reshape(owners, per_owner * width // lanes, lanes)
    arrived = lax.all_to_all(local_buffer, ("dp", "sect"), split_axis=0, concat_axis=0, tiled=True)
    own_experts = gate_weight.shape[0]
    pieces = lax.axis_size("tensor")
    inputs = (
        arrived.reshape(owners, own_experts, CAP, width)
        .transpose(1, 0, 2, 3)
        .reshape(own_experts, owners * CAP, width)
    )
    gathered = lax.all_gather(inputs, "tensor", axis=0, tiled=False)
    hidden_width = gate_weight.shape[2]
    gate_view = gate_weight.reshape(own_experts, pieces, width, hidden_width)
    up_view = up_weight.reshape(own_experts, pieces, width, hidden_width)
    gate_part = jnp.einsum(
        "tend,etdf->enf", gathered, gate_view, preferred_element_type=jnp.float32
    )
    up_part = jnp.einsum("tend,etdf->enf", gathered, up_view, preferred_element_type=jnp.float32)
    hidden = (jax.nn.silu(gate_part) * up_part).astype(jnp.bfloat16)
    out_width = down_weight.shape[2] // pieces
    down_mine = lax.all_to_all(
        down_weight.reshape(own_experts, hidden_width, pieces, out_width).transpose(2, 0, 1, 3),
        "tensor",
        split_axis=0,
        concat_axis=0,
        tiled=True,
    )
    hidden_all = lax.all_gather(hidden.transpose(0, 2, 1), "tensor", axis=0, tiled=False)
    group_sums = jnp.einsum(
        "gefn,gefc->genc", hidden_all, down_mine, preferred_element_type=jnp.float32
    ).astype(jnp.bfloat16)
    summed = jnp.sum(group_sums.astype(jnp.float32), axis=0).astype(jnp.bfloat16)
    last = summed.shape[2]
    returned = lax.all_to_all(
        summed.reshape(own_experts, owners, CAP, last)
        .transpose(1, 0, 2, 3)
        .reshape(owners, own_experts * CAP * last // lanes, lanes),
        ("dp", "sect"),
        split_axis=0,
        concat_axis=0,
        tiled=True,
    )
    expert_out = returned.reshape(slot_total, last)
    mixture = jnp.dot(combine.T, expert_out, preferred_element_type=jnp.float32).astype(
        jnp.bfloat16
    )
    attention = attend(query, cache_keys, cache_values, lengths)
    return (mixture, attention)


def solution(mesh):
    placed = (
        P(("dp", "sect"), "tensor"),
        P(("dp", "sect"), None),
        P(("dp", "sect"), None),
        P(("dp", "sect"), None, "tensor"),
        P(("dp", "sect"), None, "tensor"),
        P(("dp", "sect"), "tensor", None),
        P(("dp", "sect"), "tensor", None),
        P(("dp", "sect"), None, "tensor", None),
        P(("dp", "sect"), None, "tensor", None),
        P(("dp", "sect")),
    )
    return jax.shard_map(
        local,
        mesh=mesh,
        in_specs=placed,
        out_specs=(P(("dp", "sect"), "tensor"), P(("dp", "sect"), "tensor", None)),
        check_vma=False,
    )
```

```python
import jax
import jax.numpy as jnp
from jax import lax
from jax.sharding import PartitionSpec as P

EXPERTS = 128
CAP = 5


def route_tables(expert_ids, weights, experts, capacity):
    row_count, top_count = expert_ids.shape
    pair_count = row_count * top_count
    flat_ids = expert_ids.reshape(pair_count)
    one_hot = (flat_ids[:, None] == jnp.arange(experts, dtype=jnp.int32)[None, :]).astype(
        jnp.float32
    )
    ordinal = jnp.arange(pair_count, dtype=jnp.int32)
    earlier = (ordinal[:, None] > ordinal[None, :]).astype(jnp.float32)
    counts = jnp.dot(earlier, one_hot, preferred_element_type=jnp.float32)
    slot_index = jnp.sum(counts * one_hot, axis=1).astype(jnp.int32)
    target = flat_ids * capacity + slot_index
    select = (jnp.arange(experts * capacity, dtype=jnp.int32)[:, None] == target[None, :]).astype(
        jnp.float32
    )
    select = select.reshape(experts * capacity, row_count, top_count)
    share_norm = (weights / jnp.sum(weights, axis=1, keepdims=True)).astype(jnp.bfloat16)
    share_norm = lax.optimization_barrier(share_norm).astype(jnp.float32)
    dispatch = jnp.sum(select, axis=2).astype(jnp.bfloat16)
    combine = jnp.sum(select * share_norm[None, :, :], axis=2).astype(jnp.bfloat16)
    return (dispatch, combine)


def attend(query, cache_keys, cache_values, lengths):
    row_count, head_count, head_size = query.shape
    kv_count = cache_keys.shape[2]
    group_size = head_count // kv_count
    queries = query.reshape(row_count, kv_count, group_size, head_size)
    scores = jnp.einsum(
        "rkgd,rlkd->rkgl", queries, cache_keys, preferred_element_type=jnp.float32
    ) * head_size ** (-0.5)
    valid = jnp.arange(cache_keys.shape[1], dtype=jnp.int32)[None, :] < lengths[:, None]
    scores = jnp.where(valid[:, None, None, :], scores, -1e30)
    highest = jnp.max(scores, axis=3, keepdims=True)
    expo = jnp.exp(scores - highest)
    probs = (expo / jnp.sum(expo, axis=3, keepdims=True)).astype(jnp.bfloat16)
    result = jnp.einsum("rkgl,rlkd->rkgd", probs, cache_values, preferred_element_type=jnp.float32)
    return result.astype(jnp.bfloat16).reshape(row_count, head_count, head_size)


def shifted(x, step, count):
    return lax.ppermute(x, "tensor", perm=[(i, (i + step) % count) for i in range(count)])


def ring_projections(inputs, gate_weight, up_weight, count):
    width = inputs.shape[2]
    if count != 4:
        gathered = lax.all_gather(inputs, "tensor", axis=2, tiled=True)
        gate = jnp.einsum("end,edf->enf", gathered, gate_weight, preferred_element_type=jnp.float32)
        up = jnp.einsum("end,edf->enf", gathered, up_weight, preferred_element_type=jnp.float32)
        return gate, up
    me = lax.axis_index("tensor")
    from_left = shifted(inputs, 1, count)
    from_right = shifted(inputs, -1, count)
    half = inputs.shape[1] // 2
    far = jnp.concatenate(
        [shifted(from_right[:, :half], -1, count), shifted(from_left[:, half:], 1, count)], axis=1
    )
    gate = None
    up = None
    for piece, offset in ((inputs, 0), (from_left, count - 1), (from_right, 1), (far, 2)):
        start = ((me + offset) % count) * width
        gate_rows = lax.dynamic_slice_in_dim(gate_weight, start, width, axis=1)
        up_rows = lax.dynamic_slice_in_dim(up_weight, start, width, axis=1)
        g = jnp.einsum("end,edf->enf", piece, gate_rows, preferred_element_type=jnp.float32)
        u = jnp.einsum("end,edf->enf", piece, up_rows, preferred_element_type=jnp.float32)
        gate = g if gate is None else gate + g
        up = u if up is None else up + u
    return gate, up


def local(
    tokens,
    route_experts,
    route_weights,
    gate_weight,
    up_weight,
    down_weight,
    query,
    cache_keys,
    cache_values,
    lengths,
):
    owners = lax.axis_size("dp") * lax.axis_size("sect")
    dispatch, combine = route_tables(route_experts, route_weights, EXPERTS, CAP)
    slot_total = EXPERTS * CAP
    per_owner = slot_total // owners
    local_buffer = jnp.dot(dispatch, tokens, preferred_element_type=jnp.float32).astype(
        jnp.bfloat16
    )
    width = local_buffer.shape[1]
    lanes = 128
    local_buffer = local_buffer.reshape(owners, per_owner * width // lanes, lanes)
    arrived = lax.all_to_all(local_buffer, ("dp", "sect"), split_axis=0, concat_axis=0, tiled=True)
    own_experts = gate_weight.shape[0]
    pieces = lax.axis_size("tensor")
    inputs = (
        arrived.reshape(owners, own_experts, CAP, width)
        .transpose(1, 0, 2, 3)
        .reshape(own_experts, owners * CAP, width)
    )
    hidden_width = gate_weight.shape[2]
    gate_part, up_part = ring_projections(inputs, gate_weight, up_weight, pieces)
    hidden = (jax.nn.silu(gate_part) * up_part).astype(jnp.bfloat16)
    out_width = down_weight.shape[2] // pieces
    down_mine = lax.all_to_all(
        down_weight.reshape(own_experts, hidden_width, pieces, out_width).transpose(2, 0, 1, 3),
        "tensor",
        split_axis=0,
        concat_axis=0,
        tiled=True,
    )
    hidden_all = lax.all_gather(hidden.transpose(0, 2, 1), "tensor", axis=0, tiled=False)
    group_sums = jnp.einsum(
        "gefn,gefc->genc", hidden_all, down_mine, preferred_element_type=jnp.float32
    ).astype(jnp.bfloat16)
    summed = jnp.sum(group_sums.astype(jnp.float32), axis=0).astype(jnp.bfloat16)
    last = summed.shape[2]
    returned = lax.all_to_all(
        summed.reshape(own_experts, owners, CAP, last)
        .transpose(1, 0, 2, 3)
        .reshape(owners, own_experts * CAP * last // lanes, lanes),
        ("dp", "sect"),
        split_axis=0,
        concat_axis=0,
        tiled=True,
    )
    expert_out = returned.reshape(slot_total, last)
    mixture = jnp.dot(combine.T, expert_out, preferred_element_type=jnp.float32).astype(
        jnp.bfloat16
    )
    attention = attend(query, cache_keys, cache_values, lengths)
    return (mixture, attention)


def solution(mesh):
    placed = (
        P(("dp", "sect"), "tensor"),
        P(("dp", "sect"), None),
        P(("dp", "sect"), None),
        P(("dp", "sect"), None, "tensor"),
        P(("dp", "sect"), None, "tensor"),
        P(("dp", "sect"), "tensor", None),
        P(("dp", "sect"), "tensor", None),
        P(("dp", "sect"), None, "tensor", None),
        P(("dp", "sect"), None, "tensor", None),
        P(("dp", "sect")),
    )
    return jax.shard_map(
        local,
        mesh=mesh,
        in_specs=placed,
        out_specs=(P(("dp", "sect"), "tensor"), P(("dp", "sect"), "tensor", None)),
        check_vma=False,
    )
```

```python
import jax
import jax.numpy as jnp
from jax import lax
from jax.sharding import PartitionSpec as P

EXPERTS = 128
CAP = 5


def route_tables(expert_ids, weights, experts, capacity):
    row_count, top_count = expert_ids.shape
    pair_count = row_count * top_count
    flat_ids = expert_ids.reshape(pair_count)
    one_hot = (flat_ids[:, None] == jnp.arange(experts, dtype=jnp.int32)[None, :]).astype(
        jnp.float32
    )
    ordinal = jnp.arange(pair_count, dtype=jnp.int32)
    earlier = (ordinal[:, None] > ordinal[None, :]).astype(jnp.float32)
    counts = jnp.dot(earlier, one_hot, preferred_element_type=jnp.float32)
    slot_index = jnp.sum(counts * one_hot, axis=1).astype(jnp.int32)
    target = flat_ids * capacity + slot_index
    select = (jnp.arange(experts * capacity, dtype=jnp.int32)[:, None] == target[None, :]).astype(
        jnp.float32
    )
    select = select.reshape(experts * capacity, row_count, top_count)
    share_norm = (weights / jnp.sum(weights, axis=1, keepdims=True)).astype(jnp.bfloat16)
    share_norm = lax.optimization_barrier(share_norm).astype(jnp.float32)
    dispatch = jnp.sum(select, axis=2).astype(jnp.bfloat16)
    combine = jnp.sum(select * share_norm[None, :, :], axis=2).astype(jnp.bfloat16)
    return (dispatch, combine)


def attend(query, cache_keys, cache_values, lengths):
    row_count, head_count, head_size = query.shape
    kv_count = cache_keys.shape[2]
    group_size = head_count // kv_count
    queries = query.reshape(row_count, kv_count, group_size, head_size)
    scores = jnp.einsum(
        "rkgd,rlkd->rkgl", queries, cache_keys, preferred_element_type=jnp.float32
    ) * head_size ** (-0.5)
    valid = jnp.arange(cache_keys.shape[1], dtype=jnp.int32)[None, :] < lengths[:, None]
    scores = jnp.where(valid[:, None, None, :], scores, -1e30)
    highest = jnp.max(scores, axis=3, keepdims=True)
    expo = jnp.exp(scores - highest)
    probs = (expo / jnp.sum(expo, axis=3, keepdims=True)).astype(jnp.bfloat16)
    result = jnp.einsum("rkgl,rlkd->rkgd", probs, cache_values, preferred_element_type=jnp.float32)
    return result.astype(jnp.bfloat16).reshape(row_count, head_count, head_size)


def shifted(x, step, count):
    return lax.ppermute(x, "tensor", perm=[(i, (i + step) % count) for i in range(count)])


def ring_projections(inputs, gate_weight, up_weight, count):
    width = inputs.shape[2]
    if count != 4:
        gathered = lax.all_gather(inputs, "tensor", axis=2, tiled=True)
        gate = jnp.einsum("end,edf->enf", gathered, gate_weight, preferred_element_type=jnp.float32)
        up = jnp.einsum("end,edf->enf", gathered, up_weight, preferred_element_type=jnp.float32)
        return gate, up
    me = lax.axis_index("tensor")
    from_left = shifted(inputs, 1, count)
    from_right = shifted(inputs, -1, count)
    half = inputs.shape[1] // 2
    far = jnp.concatenate(
        [shifted(from_right[:, :half], -1, count), shifted(from_left[:, half:], 1, count)], axis=1
    )
    gate = None
    up = None
    for piece, offset in ((inputs, 0), (from_left, count - 1), (from_right, 1), (far, 2)):
        start = ((me + offset) % count) * width
        gate_rows = lax.dynamic_slice_in_dim(gate_weight, start, width, axis=1)
        up_rows = lax.dynamic_slice_in_dim(up_weight, start, width, axis=1)
        g = jnp.einsum("end,edf->enf", piece, gate_rows, preferred_element_type=jnp.float32)
        u = jnp.einsum("end,edf->enf", piece, up_rows, preferred_element_type=jnp.float32)
        gate = g if gate is None else gate + g
        up = u if up is None else up + u
    return gate, up


def split_down(down_weight, count):
    width = down_weight.shape[2] // count
    if count != 4:
        return lax.all_to_all(
            down_weight.reshape(down_weight.shape[0], down_weight.shape[1], count, width)
            .transpose(2, 0, 1, 3),
            "tensor",
            split_axis=0,
            concat_axis=0,
            tiled=True,
        )
    me = lax.axis_index("tensor")

    def columns(offset):
        start = ((me + offset) % count) * width
        return lax.dynamic_slice_in_dim(down_weight, start, width, axis=2)

    return (
        columns(0),
        shifted(columns(1), 1, count),
        shifted(columns(count - 1), -1, count),
        shifted(columns(2), 2, count),
    )


def down_projection(hidden_t, down_pieces, count):
    if count != 4:
        hidden_all = lax.all_gather(hidden_t, "tensor", axis=0, tiled=False)
        group_sums = jnp.einsum(
            "gefn,gefc->genc", hidden_all, down_pieces, preferred_element_type=jnp.float32
        ).astype(jnp.bfloat16)
        return jnp.sum(group_sums.astype(jnp.float32), axis=0).astype(jnp.bfloat16)
    from_left = shifted(hidden_t, 1, count)
    from_right = shifted(hidden_t, -1, count)
    half = hidden_t.shape[1] // 2
    far = jnp.concatenate(
        [shifted(from_right[:, :half], -1, count), shifted(from_left[:, half:], 1, count)], axis=1
    )
    total = None
    for piece, weight in zip((hidden_t, from_left, from_right, far), down_pieces):
        group = jnp.einsum("efn,efc->enc", piece, weight, preferred_element_type=jnp.float32)
        group = group.astype(jnp.bfloat16).astype(jnp.float32)
        total = group if total is None else total + group
    return total.astype(jnp.bfloat16)


def local(
    tokens,
    route_experts,
    route_weights,
    gate_weight,
    up_weight,
    down_weight,
    query,
    cache_keys,
    cache_values,
    lengths,
):
    owners = lax.axis_size("dp") * lax.axis_size("sect")
    dispatch, combine = route_tables(route_experts, route_weights, EXPERTS, CAP)
    slot_total = EXPERTS * CAP
    per_owner = slot_total // owners
    local_buffer = jnp.dot(dispatch, tokens, preferred_element_type=jnp.float32).astype(
        jnp.bfloat16
    )
    width = local_buffer.shape[1]
    lanes = 128
    local_buffer = local_buffer.reshape(owners, per_owner * width // lanes, lanes)
    pieces = lax.axis_size("tensor")
    down_pieces = split_down(down_weight, pieces)
    arrived = lax.all_to_all(local_buffer, ("dp", "sect"), split_axis=0, concat_axis=0, tiled=True)
    arrived, down_pieces = lax.optimization_barrier((arrived, down_pieces))
    own_experts = gate_weight.shape[0]
    inputs = (
        arrived.reshape(owners, own_experts, CAP, width)
        .transpose(1, 0, 2, 3)
        .reshape(own_experts, owners * CAP, width)
    )
    hidden_width = gate_weight.shape[2]
    gate_part, up_part = ring_projections(inputs, gate_weight, up_weight, pieces)
    hidden = (jax.nn.silu(gate_part) * up_part).astype(jnp.bfloat16)
    summed = down_projection(hidden.transpose(0, 2, 1), down_pieces, pieces)
    last = summed.shape[2]
    returned = lax.all_to_all(
        summed.reshape(own_experts, owners, CAP, last)
        .transpose(1, 0, 2, 3)
        .reshape(owners, own_experts * CAP * last // lanes, lanes),
        ("dp", "sect"),
        split_axis=0,
        concat_axis=0,
        tiled=True,
    )
    expert_out = returned.reshape(slot_total, last)
    mixture = jnp.dot(combine.T, expert_out, preferred_element_type=jnp.float32).astype(
        jnp.bfloat16
    )
    attention = attend(query, cache_keys, cache_values, lengths)
    return (mixture, attention)


def solution(mesh):
    placed = (
        P(("dp", "sect"), "tensor"),
        P(("dp", "sect"), None),
        P(("dp", "sect"), None),
        P(("dp", "sect"), None, "tensor"),
        P(("dp", "sect"), None, "tensor"),
        P(("dp", "sect"), "tensor", None),
        P(("dp", "sect"), "tensor", None),
        P(("dp", "sect"), None, "tensor", None),
        P(("dp", "sect"), None, "tensor", None),
        P(("dp", "sect")),
    )
    return jax.shard_map(
        local,
        mesh=mesh,
        in_specs=placed,
        out_specs=(P(("dp", "sect"), "tensor"), P(("dp", "sect"), "tensor", None)),
        check_vma=False,
    )
```

```python
import jax
import jax.numpy as jnp
from jax import lax
from jax.sharding import PartitionSpec as P

EXPERTS = 128
CAP = 5


def route_tables(expert_ids, weights, experts, capacity):
    row_count, top_count = expert_ids.shape
    pair_count = row_count * top_count
    flat_ids = expert_ids.reshape(pair_count)
    one_hot = (flat_ids[:, None] == jnp.arange(experts, dtype=jnp.int32)[None, :]).astype(
        jnp.float32
    )
    ordinal = jnp.arange(pair_count, dtype=jnp.int32)
    earlier = (ordinal[:, None] > ordinal[None, :]).astype(jnp.float32)
    counts = jnp.dot(earlier, one_hot, preferred_element_type=jnp.float32)
    slot_index = jnp.sum(counts * one_hot, axis=1).astype(jnp.int32)
    target = flat_ids * capacity + slot_index
    select = (jnp.arange(experts * capacity, dtype=jnp.int32)[:, None] == target[None, :]).astype(
        jnp.float32
    )
    select = select.reshape(experts * capacity, row_count, top_count)
    share_norm = (weights / jnp.sum(weights, axis=1, keepdims=True)).astype(jnp.bfloat16)
    share_norm = lax.optimization_barrier(share_norm).astype(jnp.float32)
    dispatch = jnp.sum(select, axis=2).astype(jnp.bfloat16)
    combine = jnp.sum(select * share_norm[None, :, :], axis=2).astype(jnp.bfloat16)
    return (dispatch, combine)


def attend(query, cache_keys, cache_values, lengths):
    row_count, head_count, head_size = query.shape
    kv_count = cache_keys.shape[2]
    group_size = head_count // kv_count
    queries = query.reshape(row_count, kv_count, group_size, head_size)
    scores = jnp.einsum(
        "rkgd,rlkd->rkgl", queries, cache_keys, preferred_element_type=jnp.float32
    ) * head_size ** (-0.5)
    valid = jnp.arange(cache_keys.shape[1], dtype=jnp.int32)[None, :] < lengths[:, None]
    scores = jnp.where(valid[:, None, None, :], scores, -1e30)
    highest = jnp.max(scores, axis=3, keepdims=True)
    expo = jnp.exp(scores - highest)
    probs = (expo / jnp.sum(expo, axis=3, keepdims=True)).astype(jnp.bfloat16)
    result = jnp.einsum("rkgl,rlkd->rkgd", probs, cache_values, preferred_element_type=jnp.float32)
    return result.astype(jnp.bfloat16).reshape(row_count, head_count, head_size)


def local(
    tokens,
    route_experts,
    route_weights,
    gate_weight,
    up_weight,
    down_weight,
    query,
    cache_keys,
    cache_values,
    lengths,
):
    owners = lax.axis_size("dp") * lax.axis_size("sect")
    dispatch, combine = route_tables(route_experts, route_weights, EXPERTS, CAP)
    slot_total = EXPERTS * CAP
    per_owner = slot_total // owners
    local_buffer = jnp.dot(dispatch, tokens, preferred_element_type=jnp.float32).astype(
        jnp.bfloat16
    )
    width = local_buffer.shape[1]
    lanes = 128
    local_buffer = local_buffer.reshape(owners, per_owner * width // lanes, lanes)
    arrived = lax.all_to_all(local_buffer, ("dp", "sect"), split_axis=0, concat_axis=0, tiled=True)
    own_experts = gate_weight.shape[0]
    pieces = lax.axis_size("tensor")
    inputs = (
        arrived.reshape(owners, own_experts, CAP, width)
        .transpose(1, 0, 2, 3)
        .reshape(own_experts, owners * CAP, width)
    )
    hidden_width = gate_weight.shape[2]
    out_width = down_weight.shape[2] // pieces
    down_split = down_weight.reshape(own_experts, hidden_width, pieces, out_width).transpose(
        2, 0, 1, 3
    )
    outgoing = jnp.concatenate(
        [jnp.broadcast_to(inputs[None], (pieces,) + inputs.shape), down_split], axis=2
    )
    incoming = lax.all_to_all(outgoing, "tensor", split_axis=0, concat_axis=0, tiled=True)
    slots = inputs.shape[1]
    gathered = incoming[:, :, :slots]
    down_mine = incoming[:, :, slots:]
    gate_view = gate_weight.reshape(own_experts, pieces, width, hidden_width)
    up_view = up_weight.reshape(own_experts, pieces, width, hidden_width)
    gate_part = jnp.einsum(
        "tend,etdf->enf", gathered, gate_view, preferred_element_type=jnp.float32
    )
    up_part = jnp.einsum("tend,etdf->enf", gathered, up_view, preferred_element_type=jnp.float32)
    hidden = (jax.nn.silu(gate_part) * up_part).astype(jnp.bfloat16)
    hidden_all = lax.all_gather(hidden.transpose(0, 2, 1), "tensor", axis=0, tiled=False)
    group_sums = jnp.einsum(
        "gefn,gefc->genc", hidden_all, down_mine, preferred_element_type=jnp.float32
    ).astype(jnp.bfloat16)
    summed = jnp.sum(group_sums.astype(jnp.float32), axis=0).astype(jnp.bfloat16)
    last = summed.shape[2]
    returned = lax.all_to_all(
        summed.reshape(own_experts, owners, CAP, last)
        .transpose(1, 0, 2, 3)
        .reshape(owners, own_experts * CAP * last // lanes, lanes),
        ("dp", "sect"),
        split_axis=0,
        concat_axis=0,
        tiled=True,
    )
    expert_out = returned.reshape(slot_total, last)
    mixture = jnp.dot(combine.T, expert_out, preferred_element_type=jnp.float32).astype(
        jnp.bfloat16
    )
    attention = attend(query, cache_keys, cache_values, lengths)
    return (mixture, attention)


def solution(mesh):
    placed = (
        P(("dp", "sect"), "tensor"),
        P(("dp", "sect"), None),
        P(("dp", "sect"), None),
        P(("dp", "sect"), None, "tensor"),
        P(("dp", "sect"), None, "tensor"),
        P(("dp", "sect"), "tensor", None),
        P(("dp", "sect"), "tensor", None),
        P(("dp", "sect"), None, "tensor", None),
        P(("dp", "sect"), None, "tensor", None),
        P(("dp", "sect")),
    )
    return jax.shard_map(
        local,
        mesh=mesh,
        in_specs=placed,
        out_specs=(P(("dp", "sect"), "tensor"), P(("dp", "sect"), "tensor", None)),
        check_vma=False,
    )
```

```python
import jax
import jax.numpy as jnp
from jax import lax
from jax.sharding import PartitionSpec as P

EXPERTS = 128
CAP = 5


def route_tables(expert_ids, weights, experts, capacity):
    row_count, top_count = expert_ids.shape
    pair_count = row_count * top_count
    flat_ids = expert_ids.reshape(pair_count)
    one_hot = (flat_ids[:, None] == jnp.arange(experts, dtype=jnp.int32)[None, :]).astype(
        jnp.float32
    )
    ordinal = jnp.arange(pair_count, dtype=jnp.int32)
    earlier = (ordinal[:, None] > ordinal[None, :]).astype(jnp.float32)
    counts = jnp.dot(earlier, one_hot, preferred_element_type=jnp.float32)
    slot_index = jnp.sum(counts * one_hot, axis=1).astype(jnp.int32)
    target = flat_ids * capacity + slot_index
    select = (jnp.arange(experts * capacity, dtype=jnp.int32)[:, None] == target[None, :]).astype(
        jnp.float32
    )
    select = select.reshape(experts * capacity, row_count, top_count)
    share_norm = (weights / jnp.sum(weights, axis=1, keepdims=True)).astype(jnp.bfloat16)
    share_norm = lax.optimization_barrier(share_norm).astype(jnp.float32)
    dispatch = jnp.sum(select, axis=2).astype(jnp.bfloat16)
    combine = jnp.sum(select * share_norm[None, :, :], axis=2).astype(jnp.bfloat16)
    return (dispatch, combine)


def attend(query, cache_keys, cache_values, lengths):
    row_count, head_count, head_size = query.shape
    kv_count = cache_keys.shape[2]
    group_size = head_count // kv_count
    queries = query.reshape(row_count, kv_count, group_size, head_size)
    scores = jnp.einsum(
        "rkgd,rlkd->rkgl", queries, cache_keys, preferred_element_type=jnp.float32
    ) * head_size ** (-0.5)
    valid = jnp.arange(cache_keys.shape[1], dtype=jnp.int32)[None, :] < lengths[:, None]
    scores = jnp.where(valid[:, None, None, :], scores, -1e30)
    highest = jnp.max(scores, axis=3, keepdims=True)
    expo = jnp.exp(scores - highest)
    probs = (expo / jnp.sum(expo, axis=3, keepdims=True)).astype(jnp.bfloat16)
    result = jnp.einsum("rkgl,rlkd->rkgd", probs, cache_values, preferred_element_type=jnp.float32)
    return result.astype(jnp.bfloat16).reshape(row_count, head_count, head_size)


def shifted(x, step, count):
    return lax.ppermute(x, "tensor", perm=[(i, (i + step) % count) for i in range(count)])


def ring_projections(inputs, gate_weight, up_weight, count):
    width = inputs.shape[2]
    if count != 4:
        gathered = lax.all_gather(inputs, "tensor", axis=2, tiled=True)
        gate = jnp.einsum("end,edf->enf", gathered, gate_weight, preferred_element_type=jnp.float32)
        up = jnp.einsum("end,edf->enf", gathered, up_weight, preferred_element_type=jnp.float32)
        return gate, up
    me = lax.axis_index("tensor")
    from_left = shifted(inputs, 1, count)
    from_right = shifted(inputs, -1, count)
    far = shifted(inputs, 2, count)
    gate = None
    up = None
    for piece, offset in ((inputs, 0), (from_left, count - 1), (from_right, 1), (far, 2)):
        start = ((me + offset) % count) * width
        gate_rows = lax.dynamic_slice_in_dim(gate_weight, start, width, axis=1)
        up_rows = lax.dynamic_slice_in_dim(up_weight, start, width, axis=1)
        g = jnp.einsum("end,edf->enf", piece, gate_rows, preferred_element_type=jnp.float32)
        u = jnp.einsum("end,edf->enf", piece, up_rows, preferred_element_type=jnp.float32)
        gate = g if gate is None else gate + g
        up = u if up is None else up + u
    return gate, up


def down_projection(hidden_t, down_mine, count):
    if count != 4:
        hidden_all = lax.all_gather(hidden_t, "tensor", axis=0, tiled=False)
        group_sums = jnp.einsum(
            "gefn,gefc->genc", hidden_all, down_mine, preferred_element_type=jnp.float32
        ).astype(jnp.bfloat16)
        return jnp.sum(group_sums.astype(jnp.float32), axis=0).astype(jnp.bfloat16)
    me = lax.axis_index("tensor")
    total = None
    for step, offset in ((0, 0), (1, count - 1), (-1, 1), (2, 2)):
        piece = hidden_t if step == 0 else shifted(hidden_t, step, count)
        weight = lax.dynamic_index_in_dim(down_mine, (me + offset) % count, axis=0, keepdims=False)
        group = jnp.einsum("efn,efc->enc", piece, weight, preferred_element_type=jnp.float32)
        group = group.astype(jnp.bfloat16).astype(jnp.float32)
        total = group if total is None else total + group
    return total.astype(jnp.bfloat16)


def local(
    tokens,
    route_experts,
    route_weights,
    gate_weight,
    up_weight,
    down_weight,
    query,
    cache_keys,
    cache_values,
    lengths,
):
    owners = lax.axis_size("dp") * lax.axis_size("sect")
    dispatch, combine = route_tables(route_experts, route_weights, EXPERTS, CAP)
    slot_total = EXPERTS * CAP
    per_owner = slot_total // owners
    local_buffer = jnp.dot(dispatch, tokens, preferred_element_type=jnp.float32).astype(
        jnp.bfloat16
    )
    width = local_buffer.shape[1]
    lanes = 128
    local_buffer = local_buffer.reshape(owners, per_owner * width // lanes, lanes)
    arrived = lax.all_to_all(local_buffer, ("dp", "sect"), split_axis=0, concat_axis=0, tiled=True)
    own_experts = gate_weight.shape[0]
    pieces = lax.axis_size("tensor")
    inputs = (
        arrived.reshape(owners, own_experts, CAP, width)
        .transpose(1, 0, 2, 3)
        .reshape(own_experts, owners * CAP, width)
    )
    hidden_width = gate_weight.shape[2]
    gate_part, up_part = ring_projections(inputs, gate_weight, up_weight, pieces)
    hidden = (jax.nn.silu(gate_part) * up_part).astype(jnp.bfloat16)
    out_width = down_weight.shape[2] // pieces
    down_mine = lax.all_to_all(
        down_weight.reshape(own_experts, hidden_width, pieces, out_width).transpose(2, 0, 1, 3),
        "tensor",
        split_axis=0,
        concat_axis=0,
        tiled=True,
    )
    summed = down_projection(hidden.transpose(0, 2, 1), down_mine, pieces)
    last = summed.shape[2]
    returned = lax.all_to_all(
        summed.reshape(own_experts, owners, CAP, last)
        .transpose(1, 0, 2, 3)
        .reshape(owners, own_experts * CAP * last // lanes, lanes),
        ("dp", "sect"),
        split_axis=0,
        concat_axis=0,
        tiled=True,
    )
    expert_out = returned.reshape(slot_total, last)
    mixture = jnp.dot(combine.T, expert_out, preferred_element_type=jnp.float32).astype(
        jnp.bfloat16
    )
    attention = attend(query, cache_keys, cache_values, lengths)
    return (mixture, attention)


def solution(mesh):
    placed = (
        P(("dp", "sect"), "tensor"),
        P(("dp", "sect"), None),
        P(("dp", "sect"), None),
        P(("dp", "sect"), None, "tensor"),
        P(("dp", "sect"), None, "tensor"),
        P(("dp", "sect"), "tensor", None),
        P(("dp", "sect"), "tensor", None),
        P(("dp", "sect"), None, "tensor", None),
        P(("dp", "sect"), None, "tensor", None),
        P(("dp", "sect")),
    )
    return jax.shard_map(
        local,
        mesh=mesh,
        in_specs=placed,
        out_specs=(P(("dp", "sect"), "tensor"), P(("dp", "sect"), "tensor", None)),
        check_vma=False,
    )
```

```python
import jax
import jax.numpy as jnp
from jax import lax
from jax.sharding import PartitionSpec as P

EXPERTS = 128
CAP = 5


def route_tables(expert_ids, weights, experts, capacity):
    row_count = expert_ids.shape[0]
    named = expert_ids[:, :, None] == jnp.arange(experts, dtype=jnp.int32)[None, None, :]
    share_norm = (weights / jnp.sum(weights, axis=1, keepdims=True)).astype(jnp.bfloat16)
    share_norm = lax.optimization_barrier(share_norm).astype(jnp.float32)
    member = jnp.sum(named.astype(jnp.float32), axis=1)
    share_of = jnp.sum(jnp.where(named, share_norm[:, :, None], 0.0), axis=1)
    rows = jnp.arange(row_count, dtype=jnp.int32)
    earlier = (rows[:, None] > rows[None, :]).astype(jnp.float32)
    slot = jnp.dot(earlier, member, preferred_element_type=jnp.float32)
    level = jnp.arange(capacity, dtype=jnp.float32)[None, :, None]
    hit = (slot.T[:, None, :] == level) & (member.T[:, None, :] > 0)
    dispatch = jnp.where(hit, 1.0, 0.0).reshape(experts * capacity, row_count)
    combine = jnp.where(hit, share_of.T[:, None, :], 0.0).reshape(experts * capacity, row_count)
    return (dispatch.astype(jnp.bfloat16), combine.astype(jnp.bfloat16))

def attend(query, cache_keys, cache_values, lengths):
    row_count, head_count, head_size = query.shape
    kv_count = cache_keys.shape[2]
    group_size = head_count // kv_count
    queries = query.reshape(row_count, kv_count, group_size, head_size)
    scores = jnp.einsum(
        "rkgd,rlkd->rkgl", queries, cache_keys, preferred_element_type=jnp.float32
    ) * head_size ** (-0.5)
    valid = jnp.arange(cache_keys.shape[1], dtype=jnp.int32)[None, :] < lengths[:, None]
    scores = jnp.where(valid[:, None, None, :], scores, -1e30)
    highest = jnp.max(scores, axis=3, keepdims=True)
    expo = jnp.exp(scores - highest)
    probs = (expo / jnp.sum(expo, axis=3, keepdims=True)).astype(jnp.bfloat16)
    result = jnp.einsum("rkgl,rlkd->rkgd", probs, cache_values, preferred_element_type=jnp.float32)
    return result.astype(jnp.bfloat16).reshape(row_count, head_count, head_size)


def shifted(x, step, count):
    return lax.ppermute(x, "tensor", perm=[(i, (i + step) % count) for i in range(count)])


def ring_projections(inputs, gate_weight, up_weight, count):
    width = inputs.shape[2]
    if count != 4:
        gathered = lax.all_gather(inputs, "tensor", axis=2, tiled=True)
        gate = jnp.einsum("end,edf->enf", gathered, gate_weight, preferred_element_type=jnp.float32)
        up = jnp.einsum("end,edf->enf", gathered, up_weight, preferred_element_type=jnp.float32)
        return gate, up
    me = lax.axis_index("tensor")
    from_left = shifted(inputs, 1, count)
    from_right = shifted(inputs, -1, count)
    half = inputs.shape[1] // 2
    far = jnp.concatenate(
        [shifted(from_right[:, :half], -1, count), shifted(from_left[:, half:], 1, count)], axis=1
    )
    gate = None
    up = None
    for piece, offset in ((inputs, 0), (from_left, count - 1), (from_right, 1), (far, 2)):
        start = ((me + offset) % count) * width
        gate_rows = lax.dynamic_slice_in_dim(gate_weight, start, width, axis=1)
        up_rows = lax.dynamic_slice_in_dim(up_weight, start, width, axis=1)
        g = jnp.einsum("end,edf->enf", piece, gate_rows, preferred_element_type=jnp.float32)
        u = jnp.einsum("end,edf->enf", piece, up_rows, preferred_element_type=jnp.float32)
        gate = g if gate is None else gate + g
        up = u if up is None else up + u
    return gate, up


def local(
    tokens,
    route_experts,
    route_weights,
    gate_weight,
    up_weight,
    down_weight,
    query,
    cache_keys,
    cache_values,
    lengths,
):
    owners = lax.axis_size("dp") * lax.axis_size("sect")
    dispatch, combine = route_tables(route_experts, route_weights, EXPERTS, CAP)
    slot_total = EXPERTS * CAP
    per_owner = slot_total // owners
    local_buffer = jnp.dot(dispatch, tokens, preferred_element_type=jnp.float32).astype(
        jnp.bfloat16
    )
    width = local_buffer.shape[1]
    lanes = 128
    local_buffer = local_buffer.reshape(owners, per_owner * width // lanes, lanes)
    arrived = lax.all_to_all(local_buffer, ("dp", "sect"), split_axis=0, concat_axis=0, tiled=True)
    own_experts = gate_weight.shape[0]
    pieces = lax.axis_size("tensor")
    inputs = (
        arrived.reshape(owners, own_experts, CAP, width)
        .transpose(1, 0, 2, 3)
        .reshape(own_experts, owners * CAP, width)
    )
    hidden_width = gate_weight.shape[2]
    gate_part, up_part = ring_projections(inputs, gate_weight, up_weight, pieces)
    hidden = (jax.nn.silu(gate_part) * up_part).astype(jnp.bfloat16)
    out_width = down_weight.shape[2] // pieces
    down_mine = lax.all_to_all(
        down_weight.reshape(own_experts, hidden_width, pieces, out_width).transpose(2, 0, 1, 3),
        "tensor",
        split_axis=0,
        concat_axis=0,
        tiled=True,
    )
    hidden_all = lax.all_gather(hidden.transpose(0, 2, 1), "tensor", axis=0, tiled=False)
    group_sums = jnp.einsum(
        "gefn,gefc->genc", hidden_all, down_mine, preferred_element_type=jnp.float32
    ).astype(jnp.bfloat16)
    summed = jnp.sum(group_sums.astype(jnp.float32), axis=0).astype(jnp.bfloat16)
    last = summed.shape[2]
    returned = lax.all_to_all(
        summed.reshape(own_experts, owners, CAP, last)
        .transpose(1, 0, 2, 3)
        .reshape(owners, own_experts * CAP * last // lanes, lanes),
        ("dp", "sect"),
        split_axis=0,
        concat_axis=0,
        tiled=True,
    )
    expert_out = returned.reshape(slot_total, last)
    mixture = jnp.dot(combine.T, expert_out, preferred_element_type=jnp.float32).astype(
        jnp.bfloat16
    )
    attention = attend(query, cache_keys, cache_values, lengths)
    return (mixture, attention)


def solution(mesh):
    placed = (
        P(("dp", "sect"), "tensor"),
        P(("dp", "sect"), None),
        P(("dp", "sect"), None),
        P(("dp", "sect"), None, "tensor"),
        P(("dp", "sect"), None, "tensor"),
        P(("dp", "sect"), "tensor", None),
        P(("dp", "sect"), "tensor", None),
        P(("dp", "sect"), None, "tensor", None),
        P(("dp", "sect"), None, "tensor", None),
        P(("dp", "sect")),
    )
    return jax.shard_map(
        local,
        mesh=mesh,
        in_specs=placed,
        out_specs=(P(("dp", "sect"), "tensor"), P(("dp", "sect"), "tensor", None)),
        check_vma=False,
    )
```

```python
import jax
import jax.numpy as jnp
from jax import lax
from jax.sharding import PartitionSpec as P

EXPERTS = 128
CAP = 5


def route_slots(expert_ids, experts, capacity):
    row_count = expert_ids.shape[0]
    named = expert_ids[:, :, None] == jnp.arange(experts, dtype=jnp.int32)[None, None, :]
    member = jnp.sum(named.astype(jnp.float32), axis=1)
    rows = jnp.arange(row_count, dtype=jnp.int32)
    earlier = (rows[:, None] > rows[None, :]).astype(jnp.float32)
    slot = jnp.dot(earlier, member, preferred_element_type=jnp.float32)
    level = jnp.arange(capacity, dtype=jnp.float32)[None, :, None]
    hit = (slot.T[:, None, :] == level) & (member.T[:, None, :] > 0)
    dispatch = jnp.where(hit, 1.0, 0.0).reshape(experts * capacity, row_count)
    return dispatch.astype(jnp.bfloat16), hit


def route_combine(expert_ids, weights, hit, experts, capacity):
    row_count = expert_ids.shape[0]
    named = expert_ids[:, :, None] == jnp.arange(experts, dtype=jnp.int32)[None, None, :]
    share_norm = (weights / jnp.sum(weights, axis=1, keepdims=True)).astype(jnp.bfloat16)
    share_norm = lax.optimization_barrier(share_norm).astype(jnp.float32)
    share_of = jnp.sum(jnp.where(named, share_norm[:, :, None], 0.0), axis=1)
    combine = jnp.where(hit, share_of.T[:, None, :], 0.0).reshape(experts * capacity, row_count)
    return combine.astype(jnp.bfloat16)

def attend(query, cache_keys, cache_values, lengths):
    row_count, head_count, head_size = query.shape
    kv_count = cache_keys.shape[2]
    group_size = head_count // kv_count
    queries = query.reshape(row_count, kv_count, group_size, head_size)
    scores = jnp.einsum(
        "rkgd,rlkd->rkgl", queries, cache_keys, preferred_element_type=jnp.float32
    ) * head_size ** (-0.5)
    valid = jnp.arange(cache_keys.shape[1], dtype=jnp.int32)[None, :] < lengths[:, None]
    scores = jnp.where(valid[:, None, None, :], scores, -1e30)
    highest = jnp.max(scores, axis=3, keepdims=True)
    expo = jnp.exp(scores - highest)
    probs = (expo / jnp.sum(expo, axis=3, keepdims=True)).astype(jnp.bfloat16)
    result = jnp.einsum("rkgl,rlkd->rkgd", probs, cache_values, preferred_element_type=jnp.float32)
    return result.astype(jnp.bfloat16).reshape(row_count, head_count, head_size)


def shifted(x, step, count):
    return lax.ppermute(x, "tensor", perm=[(i, (i + step) % count) for i in range(count)])


def ring_projections(inputs, gate_weight, up_weight, count):
    width = inputs.shape[2]
    if count != 4:
        gathered = lax.all_gather(inputs, "tensor", axis=2, tiled=True)
        gate = jnp.einsum("end,edf->enf", gathered, gate_weight, preferred_element_type=jnp.float32)
        up = jnp.einsum("end,edf->enf", gathered, up_weight, preferred_element_type=jnp.float32)
        return gate, up
    me = lax.axis_index("tensor")
    from_left = shifted(inputs, 1, count)
    from_right = shifted(inputs, -1, count)
    half = inputs.shape[1] // 2
    far = jnp.concatenate(
        [shifted(from_right[:, :half], -1, count), shifted(from_left[:, half:], 1, count)], axis=1
    )
    gate = None
    up = None
    for piece, offset in ((inputs, 0), (from_left, count - 1), (from_right, 1), (far, 2)):
        start = ((me + offset) % count) * width
        gate_rows = lax.dynamic_slice_in_dim(gate_weight, start, width, axis=1)
        up_rows = lax.dynamic_slice_in_dim(up_weight, start, width, axis=1)
        g = jnp.einsum("end,edf->enf", piece, gate_rows, preferred_element_type=jnp.float32)
        u = jnp.einsum("end,edf->enf", piece, up_rows, preferred_element_type=jnp.float32)
        gate = g if gate is None else gate + g
        up = u if up is None else up + u
    return gate, up


def local(
    tokens,
    route_experts,
    route_weights,
    gate_weight,
    up_weight,
    down_weight,
    query,
    cache_keys,
    cache_values,
    lengths,
):
    owners = lax.axis_size("dp") * lax.axis_size("sect")
    dispatch, hit = route_slots(route_experts, EXPERTS, CAP)
    slot_total = EXPERTS * CAP
    per_owner = slot_total // owners
    local_buffer = jnp.dot(dispatch, tokens, preferred_element_type=jnp.float32).astype(
        jnp.bfloat16
    )
    width = local_buffer.shape[1]
    lanes = 128
    local_buffer = local_buffer.reshape(owners, per_owner * width // lanes, lanes)
    arrived = lax.all_to_all(local_buffer, ("dp", "sect"), split_axis=0, concat_axis=0, tiled=True)
    arrived, late_ids, late_weights, late_hit = lax.optimization_barrier(
        (arrived, route_experts, route_weights, hit)
    )
    combine = route_combine(late_ids, late_weights, late_hit, EXPERTS, CAP)
    own_experts = gate_weight.shape[0]
    pieces = lax.axis_size("tensor")
    inputs = (
        arrived.reshape(owners, own_experts, CAP, width)
        .transpose(1, 0, 2, 3)
        .reshape(own_experts, owners * CAP, width)
    )
    hidden_width = gate_weight.shape[2]
    gate_part, up_part = ring_projections(inputs, gate_weight, up_weight, pieces)
    hidden = (jax.nn.silu(gate_part) * up_part).astype(jnp.bfloat16)
    out_width = down_weight.shape[2] // pieces
    down_mine = lax.all_to_all(
        down_weight.reshape(own_experts, hidden_width, pieces, out_width).transpose(2, 0, 1, 3),
        "tensor",
        split_axis=0,
        concat_axis=0,
        tiled=True,
    )
    hidden_all = lax.all_gather(hidden.transpose(0, 2, 1), "tensor", axis=0, tiled=False)
    group_sums = jnp.einsum(
        "gefn,gefc->genc", hidden_all, down_mine, preferred_element_type=jnp.float32
    ).astype(jnp.bfloat16)
    summed = jnp.sum(group_sums.astype(jnp.float32), axis=0).astype(jnp.bfloat16)
    last = summed.shape[2]
    returned = lax.all_to_all(
        summed.reshape(own_experts, owners, CAP, last)
        .transpose(1, 0, 2, 3)
        .reshape(owners, own_experts * CAP * last // lanes, lanes),
        ("dp", "sect"),
        split_axis=0,
        concat_axis=0,
        tiled=True,
    )
    expert_out = returned.reshape(slot_total, last)
    mixture = jnp.dot(combine.T, expert_out, preferred_element_type=jnp.float32).astype(
        jnp.bfloat16
    )
    attention = attend(query, cache_keys, cache_values, lengths)
    return (mixture, attention)


def solution(mesh):
    placed = (
        P(("dp", "sect"), "tensor"),
        P(("dp", "sect"), None),
        P(("dp", "sect"), None),
        P(("dp", "sect"), None, "tensor"),
        P(("dp", "sect"), None, "tensor"),
        P(("dp", "sect"), "tensor", None),
        P(("dp", "sect"), "tensor", None),
        P(("dp", "sect"), None, "tensor", None),
        P(("dp", "sect"), None, "tensor", None),
        P(("dp", "sect")),
    )
    return jax.shard_map(
        local,
        mesh=mesh,
        in_specs=placed,
        out_specs=(P(("dp", "sect"), "tensor"), P(("dp", "sect"), "tensor", None)),
        check_vma=False,
    )
```

```python
import jax
import jax.numpy as jnp
from jax import lax
from jax.sharding import PartitionSpec as P

EXPERTS = 128
CAP = 5


def route_slots(expert_ids, experts, capacity):
    row_count = expert_ids.shape[0]
    named = expert_ids[:, :, None] == jnp.arange(experts, dtype=jnp.int32)[None, None, :]
    member = jnp.sum(named.astype(jnp.float32), axis=1)
    rows = jnp.arange(row_count, dtype=jnp.int32)
    earlier = (rows[:, None] > rows[None, :]).astype(jnp.float32)
    slot = jnp.dot(earlier, member, preferred_element_type=jnp.float32)
    level = jnp.arange(capacity, dtype=jnp.float32)[None, :, None]
    hit = (slot.T[:, None, :] == level) & (member.T[:, None, :] > 0)
    dispatch = jnp.where(hit, 1.0, 0.0).reshape(experts * capacity, row_count)
    return dispatch.astype(jnp.bfloat16), hit


def route_combine(expert_ids, weights, hit, experts, capacity):
    row_count = expert_ids.shape[0]
    named = expert_ids[:, :, None] == jnp.arange(experts, dtype=jnp.int32)[None, None, :]
    share_norm = (weights / jnp.sum(weights, axis=1, keepdims=True)).astype(jnp.bfloat16)
    share_norm = lax.optimization_barrier(share_norm).astype(jnp.float32)
    share_of = jnp.sum(jnp.where(named, share_norm[:, :, None], 0.0), axis=1)
    combine = jnp.where(hit, share_of.T[:, None, :], 0.0).reshape(experts * capacity, row_count)
    return combine.astype(jnp.bfloat16)

def attend(query, cache_keys, cache_values, lengths):
    row_count, head_count, head_size = query.shape
    kv_count = cache_keys.shape[2]
    group_size = head_count // kv_count
    queries = query.reshape(row_count, kv_count, group_size, head_size)
    scores = jnp.einsum(
        "rkgd,rlkd->rkgl", queries, cache_keys, preferred_element_type=jnp.float32
    ) * head_size ** (-0.5)
    valid = jnp.arange(cache_keys.shape[1], dtype=jnp.int32)[None, :] < lengths[:, None]
    scores = jnp.where(valid[:, None, None, :], scores, -1e30)
    highest = jnp.max(scores, axis=3, keepdims=True)
    expo = jnp.exp(scores - highest)
    probs = (expo / jnp.sum(expo, axis=3, keepdims=True)).astype(jnp.bfloat16)
    result = jnp.einsum("rkgl,rlkd->rkgd", probs, cache_values, preferred_element_type=jnp.float32)
    return result.astype(jnp.bfloat16).reshape(row_count, head_count, head_size)


def shifted(x, step, count):
    return lax.ppermute(x, "tensor", perm=[(i, (i + step) % count) for i in range(count)])


def ring_projections(inputs, gate_weight, up_weight, count):
    width = inputs.shape[2]
    if count != 4:
        gathered = lax.all_gather(inputs, "tensor", axis=2, tiled=True)
        gate = jnp.einsum("end,edf->enf", gathered, gate_weight, preferred_element_type=jnp.float32)
        up = jnp.einsum("end,edf->enf", gathered, up_weight, preferred_element_type=jnp.float32)
        return gate, up
    me = lax.axis_index("tensor")
    from_left = shifted(inputs, 1, count)
    from_right = shifted(inputs, -1, count)
    half = inputs.shape[1] // 2
    far = jnp.concatenate(
        [shifted(from_right[:, :half], -1, count), shifted(from_left[:, half:], 1, count)], axis=1
    )
    gate = None
    up = None
    for piece, offset in ((inputs, 0), (from_left, count - 1), (from_right, 1), (far, 2)):
        start = ((me + offset) % count) * width
        gate_rows = lax.dynamic_slice_in_dim(gate_weight, start, width, axis=1)
        up_rows = lax.dynamic_slice_in_dim(up_weight, start, width, axis=1)
        g = jnp.einsum("end,edf->enf", piece, gate_rows, preferred_element_type=jnp.float32)
        u = jnp.einsum("end,edf->enf", piece, up_rows, preferred_element_type=jnp.float32)
        gate = g if gate is None else gate + g
        up = u if up is None else up + u
    return gate, up


def split_down(down_weight, count):
    width = down_weight.shape[2] // count
    if count != 4:
        return lax.all_to_all(
            down_weight.reshape(down_weight.shape[0], down_weight.shape[1], count, width)
            .transpose(2, 0, 1, 3),
            "tensor",
            split_axis=0,
            concat_axis=0,
            tiled=True,
        )
    me = lax.axis_index("tensor")

    def columns(offset):
        start = ((me + offset) % count) * width
        return lax.dynamic_slice_in_dim(down_weight, start, width, axis=2)

    return (
        columns(0),
        shifted(columns(1), 1, count),
        shifted(columns(count - 1), -1, count),
        shifted(columns(2), 2, count),
    )


def down_projection(hidden_t, down_pieces, count):
    hidden_all = lax.all_gather(hidden_t, "tensor", axis=0, tiled=False)
    if count != 4:
        group_sums = jnp.einsum(
            "gefn,gefc->genc", hidden_all, down_pieces, preferred_element_type=jnp.float32
        ).astype(jnp.bfloat16)
        return jnp.sum(group_sums.astype(jnp.float32), axis=0).astype(jnp.bfloat16)
    me = lax.axis_index("tensor")
    total = None
    for offset, weight in zip((0, count - 1, 1, 2), down_pieces):
        piece = lax.dynamic_index_in_dim(hidden_all, (me + offset) % count, axis=0, keepdims=False)
        group = jnp.einsum("efn,efc->enc", piece, weight, preferred_element_type=jnp.float32)
        group = group.astype(jnp.bfloat16).astype(jnp.float32)
        total = group if total is None else total + group
    return total.astype(jnp.bfloat16)


def local(
    tokens,
    route_experts,
    route_weights,
    gate_weight,
    up_weight,
    down_weight,
    query,
    cache_keys,
    cache_values,
    lengths,
):
    owners = lax.axis_size("dp") * lax.axis_size("sect")
    dispatch, hit = route_slots(route_experts, EXPERTS, CAP)
    slot_total = EXPERTS * CAP
    per_owner = slot_total // owners
    local_buffer = jnp.dot(dispatch, tokens, preferred_element_type=jnp.float32).astype(
        jnp.bfloat16
    )
    width = local_buffer.shape[1]
    lanes = 128
    local_buffer = local_buffer.reshape(owners, per_owner * width // lanes, lanes)
    down_pieces = split_down(down_weight, lax.axis_size("tensor"))
    arrived = lax.all_to_all(local_buffer, ("dp", "sect"), split_axis=0, concat_axis=0, tiled=True)
    arrived, late_ids, late_weights, late_hit, down_pieces = lax.optimization_barrier(
        (arrived, route_experts, route_weights, hit, down_pieces)
    )
    combine = route_combine(late_ids, late_weights, late_hit, EXPERTS, CAP)
    own_experts = gate_weight.shape[0]
    pieces = lax.axis_size("tensor")
    inputs = (
        arrived.reshape(owners, own_experts, CAP, width)
        .transpose(1, 0, 2, 3)
        .reshape(own_experts, owners * CAP, width)
    )
    hidden_width = gate_weight.shape[2]
    gate_part, up_part = ring_projections(inputs, gate_weight, up_weight, pieces)
    hidden = (jax.nn.silu(gate_part) * up_part).astype(jnp.bfloat16)
    summed = down_projection(hidden.transpose(0, 2, 1), down_pieces, pieces)
    last = summed.shape[2]
    returned = lax.all_to_all(
        summed.reshape(own_experts, owners, CAP, last)
        .transpose(1, 0, 2, 3)
        .reshape(owners, own_experts * CAP * last // lanes, lanes),
        ("dp", "sect"),
        split_axis=0,
        concat_axis=0,
        tiled=True,
    )
    expert_out = returned.reshape(slot_total, last)
    mixture = jnp.dot(combine.T, expert_out, preferred_element_type=jnp.float32).astype(
        jnp.bfloat16
    )
    attention = attend(query, cache_keys, cache_values, lengths)
    return (mixture, attention)


def solution(mesh):
    placed = (
        P(("dp", "sect"), "tensor"),
        P(("dp", "sect"), None),
        P(("dp", "sect"), None),
        P(("dp", "sect"), None, "tensor"),
        P(("dp", "sect"), None, "tensor"),
        P(("dp", "sect"), "tensor", None),
        P(("dp", "sect"), "tensor", None),
        P(("dp", "sect"), None, "tensor", None),
        P(("dp", "sect"), None, "tensor", None),
        P(("dp", "sect")),
    )
    return jax.shard_map(
        local,
        mesh=mesh,
        in_specs=placed,
        out_specs=(P(("dp", "sect"), "tensor"), P(("dp", "sect"), "tensor", None)),
        check_vma=False,
    )
```

```python
import jax
import jax.numpy as jnp
from jax import lax
from jax.sharding import PartitionSpec as P

EXPERTS = 128
CAP = 5


def route_slots(expert_ids, experts, capacity):
    row_count = expert_ids.shape[0]
    named = expert_ids[:, :, None] == jnp.arange(experts, dtype=jnp.int32)[None, None, :]
    member = jnp.sum(named.astype(jnp.float32), axis=1)
    rows = jnp.arange(row_count, dtype=jnp.int32)
    earlier = (rows[:, None] > rows[None, :]).astype(jnp.float32)
    slot = jnp.dot(earlier, member, preferred_element_type=jnp.float32)
    level = jnp.arange(capacity, dtype=jnp.float32)[None, :, None]
    hit = (slot.T[:, None, :] == level) & (member.T[:, None, :] > 0)
    dispatch = jnp.where(hit, 1.0, 0.0).reshape(experts * capacity, row_count)
    return dispatch.astype(jnp.bfloat16), hit


def route_combine(expert_ids, weights, hit, experts, capacity):
    row_count = expert_ids.shape[0]
    named = expert_ids[:, :, None] == jnp.arange(experts, dtype=jnp.int32)[None, None, :]
    share_norm = (weights / jnp.sum(weights, axis=1, keepdims=True)).astype(jnp.bfloat16)
    share_norm = lax.optimization_barrier(share_norm).astype(jnp.float32)
    share_of = jnp.sum(jnp.where(named, share_norm[:, :, None], 0.0), axis=1)
    combine = jnp.where(hit, share_of.T[:, None, :], 0.0).reshape(experts * capacity, row_count)
    return combine.astype(jnp.bfloat16)

def attend(query, cache_keys, cache_values, lengths):
    row_count, head_count, head_size = query.shape
    kv_count = cache_keys.shape[2]
    group_size = head_count // kv_count
    queries = query.reshape(row_count, kv_count, group_size, head_size)
    scores = jnp.einsum(
        "rkgd,rlkd->rkgl", queries, cache_keys, preferred_element_type=jnp.float32
    ) * head_size ** (-0.5)
    valid = jnp.arange(cache_keys.shape[1], dtype=jnp.int32)[None, :] < lengths[:, None]
    scores = jnp.where(valid[:, None, None, :], scores, -1e30)
    highest = jnp.max(scores, axis=3, keepdims=True)
    expo = jnp.exp(scores - highest)
    probs = (expo / jnp.sum(expo, axis=3, keepdims=True)).astype(jnp.bfloat16)
    result = jnp.einsum("rkgl,rlkd->rkgd", probs, cache_values, preferred_element_type=jnp.float32)
    return result.astype(jnp.bfloat16).reshape(row_count, head_count, head_size)


def shifted(x, step, count):
    return lax.ppermute(x, "tensor", perm=[(i, (i + step) % count) for i in range(count)])


def ring_projections(inputs, gate_weight, up_weight, count):
    width = inputs.shape[2]
    if count != 4:
        gathered = lax.all_gather(inputs, "tensor", axis=2, tiled=True)
        gate = jnp.einsum("end,edf->enf", gathered, gate_weight, preferred_element_type=jnp.float32)
        up = jnp.einsum("end,edf->enf", gathered, up_weight, preferred_element_type=jnp.float32)
        return gate, up
    me = lax.axis_index("tensor")
    half = inputs.shape[1] // 2
    top, bottom = inputs[:, :half], inputs[:, half:]
    right_top = shifted(top, -1, count)
    left_bottom = shifted(bottom, 1, count)
    from_left = jnp.concatenate([shifted(top, 1, count), left_bottom], axis=1)
    from_right = jnp.concatenate([right_top, shifted(bottom, -1, count)], axis=1)
    far = jnp.concatenate([shifted(right_top, -1, count), shifted(left_bottom, 1, count)], axis=1)
    gate = None
    up = None
    for piece, offset in ((inputs, 0), (from_left, count - 1), (from_right, 1), (far, 2)):
        start = ((me + offset) % count) * width
        gate_rows = lax.dynamic_slice_in_dim(gate_weight, start, width, axis=1)
        up_rows = lax.dynamic_slice_in_dim(up_weight, start, width, axis=1)
        g = jnp.einsum("end,edf->enf", piece, gate_rows, preferred_element_type=jnp.float32)
        u = jnp.einsum("end,edf->enf", piece, up_rows, preferred_element_type=jnp.float32)
        gate = g if gate is None else gate + g
        up = u if up is None else up + u
    return gate, up


def split_down(down_weight, count):
    width = down_weight.shape[2] // count
    if count != 4:
        return lax.all_to_all(
            down_weight.reshape(down_weight.shape[0], down_weight.shape[1], count, width)
            .transpose(2, 0, 1, 3),
            "tensor",
            split_axis=0,
            concat_axis=0,
            tiled=True,
        )
    me = lax.axis_index("tensor")

    def columns(offset):
        start = ((me + offset) % count) * width
        return lax.dynamic_slice_in_dim(down_weight, start, width, axis=2)

    return (
        columns(0),
        shifted(columns(1), 1, count),
        shifted(columns(count - 1), -1, count),
        shifted(columns(2), 2, count),
    )


def down_projection(hidden_t, down_pieces, count):
    hidden_all = lax.all_gather(hidden_t, "tensor", axis=0, tiled=False)
    if count != 4:
        group_sums = jnp.einsum(
            "gefn,gefc->genc", hidden_all, down_pieces, preferred_element_type=jnp.float32
        ).astype(jnp.bfloat16)
        return jnp.sum(group_sums.astype(jnp.float32), axis=0).astype(jnp.bfloat16)
    me = lax.axis_index("tensor")
    total = None
    for offset, weight in zip((0, count - 1, 1, 2), down_pieces):
        piece = lax.dynamic_index_in_dim(hidden_all, (me + offset) % count, axis=0, keepdims=False)
        group = jnp.einsum("efn,efc->enc", piece, weight, preferred_element_type=jnp.float32)
        group = group.astype(jnp.bfloat16).astype(jnp.float32)
        total = group if total is None else total + group
    return total.astype(jnp.bfloat16)


def local(
    tokens,
    route_experts,
    route_weights,
    gate_weight,
    up_weight,
    down_weight,
    query,
    cache_keys,
    cache_values,
    lengths,
):
    owners = lax.axis_size("dp") * lax.axis_size("sect")
    dispatch, hit = route_slots(route_experts, EXPERTS, CAP)
    slot_total = EXPERTS * CAP
    per_owner = slot_total // owners
    local_buffer = jnp.dot(dispatch, tokens, preferred_element_type=jnp.float32).astype(
        jnp.bfloat16
    )
    width = local_buffer.shape[1]
    lanes = 128
    local_buffer = local_buffer.reshape(owners, per_owner * width // lanes, lanes)
    down_pieces = split_down(down_weight, lax.axis_size("tensor"))
    arrived = lax.all_to_all(local_buffer, ("dp", "sect"), split_axis=0, concat_axis=0, tiled=True)
    arrived, late_ids, late_weights, late_hit, down_pieces = lax.optimization_barrier(
        (arrived, route_experts, route_weights, hit, down_pieces)
    )
    combine = route_combine(late_ids, late_weights, late_hit, EXPERTS, CAP)
    own_experts = gate_weight.shape[0]
    pieces = lax.axis_size("tensor")
    inputs = (
        arrived.reshape(owners, own_experts, CAP, width)
        .transpose(1, 0, 2, 3)
        .reshape(own_experts, owners * CAP, width)
    )
    hidden_width = gate_weight.shape[2]
    gate_part, up_part = ring_projections(inputs, gate_weight, up_weight, pieces)
    hidden = (jax.nn.silu(gate_part) * up_part).astype(jnp.bfloat16)
    summed = down_projection(hidden.transpose(0, 2, 1), down_pieces, pieces)
    last = summed.shape[2]
    returned = lax.all_to_all(
        summed.reshape(own_experts, owners, CAP, last)
        .transpose(1, 0, 2, 3)
        .reshape(owners, own_experts * CAP * last // lanes, lanes),
        ("dp", "sect"),
        split_axis=0,
        concat_axis=0,
        tiled=True,
    )
    expert_out = returned.reshape(slot_total, last)
    mixture = jnp.dot(combine.T, expert_out, preferred_element_type=jnp.float32).astype(
        jnp.bfloat16
    )
    attention = attend(query, cache_keys, cache_values, lengths)
    return (mixture, attention)


def solution(mesh):
    placed = (
        P(("dp", "sect"), "tensor"),
        P(("dp", "sect"), None),
        P(("dp", "sect"), None),
        P(("dp", "sect"), None, "tensor"),
        P(("dp", "sect"), None, "tensor"),
        P(("dp", "sect"), "tensor", None),
        P(("dp", "sect"), "tensor", None),
        P(("dp", "sect"), None, "tensor", None),
        P(("dp", "sect"), None, "tensor", None),
        P(("dp", "sect")),
    )
    return jax.shard_map(
        local,
        mesh=mesh,
        in_specs=placed,
        out_specs=(P(("dp", "sect"), "tensor"), P(("dp", "sect"), "tensor", None)),
        check_vma=False,
    )
```

```python
import jax
import jax.numpy as jnp
from jax import lax
from jax.sharding import PartitionSpec as P

EXPERTS = 128
CAP = 5


def route_slots(expert_ids, experts, capacity):
    row_count = expert_ids.shape[0]
    named = expert_ids.T[:, :, None] == jnp.arange(experts, dtype=jnp.int32)[None, None, :]
    member = jnp.sum(named.astype(jnp.float32), axis=0)
    rows = jnp.arange(row_count, dtype=jnp.int32)
    earlier = (rows[:, None] > rows[None, :]).astype(jnp.float32)
    slot = jnp.dot(earlier, member, preferred_element_type=jnp.float32)
    level = jnp.arange(capacity, dtype=jnp.float32)[None, :, None]
    hit = (slot.T[:, None, :] == level) & (member.T[:, None, :] > 0)
    dispatch = jnp.where(hit, 1.0, 0.0).reshape(experts * capacity, row_count)
    return dispatch.astype(jnp.bfloat16), hit


def route_combine(expert_ids, weights, hit, experts, capacity):
    row_count = expert_ids.shape[0]
    named = expert_ids[:, :, None] == jnp.arange(experts, dtype=jnp.int32)[None, None, :]
    share_norm = (weights / jnp.sum(weights, axis=1, keepdims=True)).astype(jnp.bfloat16)
    share_norm = lax.optimization_barrier(share_norm).astype(jnp.float32)
    share_of = jnp.sum(jnp.where(named, share_norm[:, :, None], 0.0), axis=1)
    combine = jnp.where(hit, share_of.T[:, None, :], 0.0).reshape(experts * capacity, row_count)
    return combine.astype(jnp.bfloat16)

def attend(query, cache_keys, cache_values, lengths):
    row_count, head_count, head_size = query.shape
    kv_count = cache_keys.shape[2]
    group_size = head_count // kv_count
    queries = query.reshape(row_count, kv_count, group_size, head_size)
    scores = jnp.einsum(
        "rkgd,rlkd->rkgl", queries, cache_keys, preferred_element_type=jnp.float32
    ) * head_size ** (-0.5)
    valid = jnp.arange(cache_keys.shape[1], dtype=jnp.int32)[None, :] < lengths[:, None]
    scores = jnp.where(valid[:, None, None, :], scores, -1e30)
    highest = jnp.max(scores, axis=3, keepdims=True)
    expo = jnp.exp(scores - highest)
    probs = (expo / jnp.sum(expo, axis=3, keepdims=True)).astype(jnp.bfloat16)
    result = jnp.einsum("rkgl,rlkd->rkgd", probs, cache_values, preferred_element_type=jnp.float32)
    return result.astype(jnp.bfloat16).reshape(row_count, head_count, head_size)


def shifted(x, step, count):
    return lax.ppermute(x, "tensor", perm=[(i, (i + step) % count) for i in range(count)])


def ring_projections(inputs, gate_weight, up_weight, count):
    width = inputs.shape[2]
    if count != 4:
        gathered = lax.all_gather(inputs, "tensor", axis=2, tiled=True)
        gate = jnp.einsum("end,edf->enf", gathered, gate_weight, preferred_element_type=jnp.float32)
        up = jnp.einsum("end,edf->enf", gathered, up_weight, preferred_element_type=jnp.float32)
        return gate, up
    me = lax.axis_index("tensor")
    half = inputs.shape[1] // 2
    top, bottom = inputs[:, :half], inputs[:, half:]
    right_top = shifted(top, -1, count)
    left_bottom = shifted(bottom, 1, count)
    from_left = jnp.concatenate([shifted(top, 1, count), left_bottom], axis=1)
    from_right = jnp.concatenate([right_top, shifted(bottom, -1, count)], axis=1)
    far = jnp.concatenate([shifted(right_top, -1, count), shifted(left_bottom, 1, count)], axis=1)
    gate = None
    up = None
    for piece, offset in ((inputs, 0), (from_left, count - 1), (from_right, 1), (far, 2)):
        start = ((me + offset) % count) * width
        gate_rows = lax.dynamic_slice_in_dim(gate_weight, start, width, axis=1)
        up_rows = lax.dynamic_slice_in_dim(up_weight, start, width, axis=1)
        g = jnp.einsum("end,edf->enf", piece, gate_rows, preferred_element_type=jnp.float32)
        u = jnp.einsum("end,edf->enf", piece, up_rows, preferred_element_type=jnp.float32)
        gate = g if gate is None else gate + g
        up = u if up is None else up + u
    return gate, up


def split_down(down_weight, count):
    width = down_weight.shape[2] // count
    if count != 4:
        return lax.all_to_all(
            down_weight.reshape(down_weight.shape[0], down_weight.shape[1], count, width)
            .transpose(2, 0, 1, 3),
            "tensor",
            split_axis=0,
            concat_axis=0,
            tiled=True,
        )
    me = lax.axis_index("tensor")

    def columns(offset):
        start = ((me + offset) % count) * width
        return lax.dynamic_slice_in_dim(down_weight, start, width, axis=2)

    return (
        columns(0),
        shifted(columns(1), 1, count),
        shifted(columns(count - 1), -1, count),
        shifted(columns(2), 2, count),
    )


def down_projection(hidden_t, down_pieces, count):
    hidden_all = lax.all_gather(hidden_t, "tensor", axis=0, tiled=False)
    if count != 4:
        group_sums = jnp.einsum(
            "gefn,gefc->genc", hidden_all, down_pieces, preferred_element_type=jnp.float32
        ).astype(jnp.bfloat16)
        return jnp.sum(group_sums.astype(jnp.float32), axis=0).astype(jnp.bfloat16)
    me = lax.axis_index("tensor")
    total = None
    for offset, weight in zip((0, count - 1, 1, 2), down_pieces):
        piece = lax.dynamic_index_in_dim(hidden_all, (me + offset) % count, axis=0, keepdims=False)
        group = jnp.einsum("efn,efc->enc", piece, weight, preferred_element_type=jnp.float32)
        group = group.astype(jnp.bfloat16).astype(jnp.float32)
        total = group if total is None else total + group
    return total.astype(jnp.bfloat16)


def local(
    tokens,
    route_experts,
    route_weights,
    gate_weight,
    up_weight,
    down_weight,
    query,
    cache_keys,
    cache_values,
    lengths,
):
    owners = lax.axis_size("dp") * lax.axis_size("sect")
    dispatch, hit = route_slots(route_experts, EXPERTS, CAP)
    slot_total = EXPERTS * CAP
    per_owner = slot_total // owners
    local_buffer = jnp.dot(dispatch, tokens, preferred_element_type=jnp.float32).astype(
        jnp.bfloat16
    )
    width = local_buffer.shape[1]
    lanes = 128
    local_buffer = local_buffer.reshape(owners, per_owner * width // lanes, lanes)
    down_pieces = split_down(down_weight, lax.axis_size("tensor"))
    arrived = lax.all_to_all(local_buffer, ("dp", "sect"), split_axis=0, concat_axis=0, tiled=True)
    arrived, late_ids, late_weights, late_hit, down_pieces = lax.optimization_barrier(
        (arrived, route_experts, route_weights, hit, down_pieces)
    )
    combine = route_combine(late_ids, late_weights, late_hit, EXPERTS, CAP)
    own_experts = gate_weight.shape[0]
    pieces = lax.axis_size("tensor")
    inputs = (
        arrived.reshape(owners, own_experts, CAP, width)
        .transpose(1, 0, 2, 3)
        .reshape(own_experts, owners * CAP, width)
    )
    hidden_width = gate_weight.shape[2]
    gate_part, up_part = ring_projections(inputs, gate_weight, up_weight, pieces)
    hidden = (jax.nn.silu(gate_part) * up_part).astype(jnp.bfloat16)
    summed = down_projection(hidden.transpose(0, 2, 1), down_pieces, pieces)
    last = summed.shape[2]
    returned = lax.all_to_all(
        summed.reshape(own_experts, owners, CAP, last)
        .transpose(1, 0, 2, 3)
        .reshape(owners, own_experts * CAP * last // lanes, lanes),
        ("dp", "sect"),
        split_axis=0,
        concat_axis=0,
        tiled=True,
    )
    expert_out = returned.reshape(slot_total, last)
    mixture = jnp.dot(combine.T, expert_out, preferred_element_type=jnp.float32).astype(
        jnp.bfloat16
    )
    attention = attend(query, cache_keys, cache_values, lengths)
    return (mixture, attention)


def solution(mesh):
    placed = (
        P(("dp", "sect"), "tensor"),
        P(("dp", "sect"), None),
        P(("dp", "sect"), None),
        P(("dp", "sect"), None, "tensor"),
        P(("dp", "sect"), None, "tensor"),
        P(("dp", "sect"), "tensor", None),
        P(("dp", "sect"), "tensor", None),
        P(("dp", "sect"), None, "tensor", None),
        P(("dp", "sect"), None, "tensor", None),
        P(("dp", "sect")),
    )
    return jax.shard_map(
        local,
        mesh=mesh,
        in_specs=placed,
        out_specs=(P(("dp", "sect"), "tensor"), P(("dp", "sect"), "tensor", None)),
        check_vma=False,
    )
```

```python
import jax
import jax.numpy as jnp
from jax import lax
from jax.sharding import PartitionSpec as P

EXPERTS = 128
CAP = 5


def route_slots(expert_ids, experts, capacity):
    row_count = expert_ids.shape[0]
    named = expert_ids[:, :, None] == jnp.arange(experts, dtype=jnp.int32)[None, None, :]
    member = jnp.sum(named.astype(jnp.float32), axis=1)
    rows = jnp.arange(row_count, dtype=jnp.int32)
    earlier = (rows[:, None] > rows[None, :]).astype(jnp.float32)
    slot = jnp.dot(earlier, member, preferred_element_type=jnp.float32)
    level = jnp.arange(capacity, dtype=jnp.float32)[None, :, None]
    hit = (slot.T[:, None, :] == level) & (member.T[:, None, :] > 0)
    dispatch = jnp.where(hit, 1.0, 0.0).reshape(experts * capacity, row_count)
    return dispatch.astype(jnp.bfloat16), hit


def route_combine(expert_ids, weights, hit, experts, capacity):
    row_count = expert_ids.shape[0]
    named = expert_ids[:, :, None] == jnp.arange(experts, dtype=jnp.int32)[None, None, :]
    share_norm = (weights / jnp.sum(weights, axis=1, keepdims=True)).astype(jnp.bfloat16)
    share_norm = lax.optimization_barrier(share_norm).astype(jnp.float32)
    share_of = jnp.sum(jnp.where(named, share_norm[:, :, None], 0.0), axis=1)
    combine = jnp.where(hit, share_of.T[:, None, :], 0.0).reshape(experts * capacity, row_count)
    return combine.astype(jnp.bfloat16)

def attend(query, cache_keys, cache_values, lengths):
    row_count, head_count, head_size = query.shape
    kv_count = cache_keys.shape[2]
    group_size = head_count // kv_count
    queries = query.reshape(row_count, kv_count, group_size, head_size)
    scores = jnp.einsum(
        "rkgd,rlkd->rkgl", queries, cache_keys, preferred_element_type=jnp.float32
    ) * head_size ** (-0.5)
    valid = jnp.arange(cache_keys.shape[1], dtype=jnp.int32)[None, :] < lengths[:, None]
    scores = jnp.where(valid[:, None, None, :], scores, -1e30)
    highest = jnp.max(scores, axis=3, keepdims=True)
    expo = jnp.exp(scores - highest)
    probs = (expo / jnp.sum(expo, axis=3, keepdims=True)).astype(jnp.bfloat16)
    result = jnp.einsum("rkgl,rlkd->rkgd", probs, cache_values, preferred_element_type=jnp.float32)
    return result.astype(jnp.bfloat16).reshape(row_count, head_count, head_size)


def shifted(x, step, count):
    return lax.ppermute(x, "tensor", perm=[(i, (i + step) % count) for i in range(count)])


def ring_projections(inputs, gate_weight, up_weight, count):
    width = inputs.shape[2]
    if count != 4:
        gathered = lax.all_gather(inputs, "tensor", axis=2, tiled=True)
        gate = jnp.einsum("end,edf->enf", gathered, gate_weight, preferred_element_type=jnp.float32)
        up = jnp.einsum("end,edf->enf", gathered, up_weight, preferred_element_type=jnp.float32)
        return gate, up
    me = lax.axis_index("tensor")
    half = inputs.shape[1] // 2
    top, bottom = inputs[:, :half], inputs[:, half:]
    right_top = shifted(top, -1, count)
    from_left = shifted(inputs, 1, count)
    left_bottom = from_left[:, half:]
    from_right = jnp.concatenate([right_top, shifted(bottom, -1, count)], axis=1)
    far = jnp.concatenate([shifted(right_top, -1, count), shifted(left_bottom, 1, count)], axis=1)
    gate = None
    up = None
    for piece, offset in ((inputs, 0), (from_left, count - 1), (from_right, 1), (far, 2)):
        start = ((me + offset) % count) * width
        gate_rows = lax.dynamic_slice_in_dim(gate_weight, start, width, axis=1)
        up_rows = lax.dynamic_slice_in_dim(up_weight, start, width, axis=1)
        g = jnp.einsum("end,edf->enf", piece, gate_rows, preferred_element_type=jnp.float32)
        u = jnp.einsum("end,edf->enf", piece, up_rows, preferred_element_type=jnp.float32)
        gate = g if gate is None else gate + g
        up = u if up is None else up + u
    return gate, up


def split_down(down_weight, count):
    width = down_weight.shape[2] // count
    if count != 4:
        return lax.all_to_all(
            down_weight.reshape(down_weight.shape[0], down_weight.shape[1], count, width)
            .transpose(2, 0, 1, 3),
            "tensor",
            split_axis=0,
            concat_axis=0,
            tiled=True,
        )
    me = lax.axis_index("tensor")

    def columns(offset):
        start = ((me + offset) % count) * width
        return lax.dynamic_slice_in_dim(down_weight, start, width, axis=2)

    return (
        columns(0),
        shifted(columns(1), 1, count),
        shifted(columns(count - 1), -1, count),
        shifted(columns(2), 2, count),
    )


def down_projection(hidden_t, down_pieces, count):
    hidden_all = lax.all_gather(hidden_t, "tensor", axis=0, tiled=False)
    if count != 4:
        group_sums = jnp.einsum(
            "gefn,gefc->genc", hidden_all, down_pieces, preferred_element_type=jnp.float32
        ).astype(jnp.bfloat16)
        return jnp.sum(group_sums.astype(jnp.float32), axis=0).astype(jnp.bfloat16)
    me = lax.axis_index("tensor")
    total = None
    for offset, weight in zip((0, count - 1, 1, 2), down_pieces):
        piece = lax.dynamic_index_in_dim(hidden_all, (me + offset) % count, axis=0, keepdims=False)
        group = jnp.einsum("efn,efc->enc", piece, weight, preferred_element_type=jnp.float32)
        group = group.astype(jnp.bfloat16).astype(jnp.float32)
        total = group if total is None else total + group
    return total.astype(jnp.bfloat16)


def local(
    tokens,
    route_experts,
    route_weights,
    gate_weight,
    up_weight,
    down_weight,
    query,
    cache_keys,
    cache_values,
    lengths,
):
    owners = lax.axis_size("dp") * lax.axis_size("sect")
    dispatch, hit = route_slots(route_experts, EXPERTS, CAP)
    slot_total = EXPERTS * CAP
    per_owner = slot_total // owners
    local_buffer = jnp.dot(dispatch, tokens, preferred_element_type=jnp.float32).astype(
        jnp.bfloat16
    )
    width = local_buffer.shape[1]
    lanes = 128
    local_buffer = local_buffer.reshape(owners, per_owner * width // lanes, lanes)
    down_pieces = split_down(down_weight, lax.axis_size("tensor"))
    arrived = lax.all_to_all(local_buffer, ("dp", "sect"), split_axis=0, concat_axis=0, tiled=True)
    arrived, late_ids, late_weights, late_hit, down_pieces = lax.optimization_barrier(
        (arrived, route_experts, route_weights, hit, down_pieces)
    )
    combine = route_combine(late_ids, late_weights, late_hit, EXPERTS, CAP)
    own_experts = gate_weight.shape[0]
    pieces = lax.axis_size("tensor")
    inputs = (
        arrived.reshape(owners, own_experts, CAP, width)
        .transpose(1, 0, 2, 3)
        .reshape(own_experts, owners * CAP, width)
    )
    hidden_width = gate_weight.shape[2]
    gate_part, up_part = ring_projections(inputs, gate_weight, up_weight, pieces)
    hidden = (jax.nn.silu(gate_part) * up_part).astype(jnp.bfloat16)
    summed = down_projection(hidden.transpose(0, 2, 1), down_pieces, pieces)
    last = summed.shape[2]
    returned = lax.all_to_all(
        summed.reshape(own_experts, owners, CAP, last)
        .transpose(1, 0, 2, 3)
        .reshape(owners, own_experts * CAP * last // lanes, lanes),
        ("dp", "sect"),
        split_axis=0,
        concat_axis=0,
        tiled=True,
    )
    expert_out = returned.reshape(slot_total, last)
    mixture = jnp.dot(combine.T, expert_out, preferred_element_type=jnp.float32).astype(
        jnp.bfloat16
    )
    attention = attend(query, cache_keys, cache_values, lengths)
    return (mixture, attention)


def solution(mesh):
    placed = (
        P(("dp", "sect"), "tensor"),
        P(("dp", "sect"), None),
        P(("dp", "sect"), None),
        P(("dp", "sect"), None, "tensor"),
        P(("dp", "sect"), None, "tensor"),
        P(("dp", "sect"), "tensor", None),
        P(("dp", "sect"), "tensor", None),
        P(("dp", "sect"), None, "tensor", None),
        P(("dp", "sect"), None, "tensor", None),
        P(("dp", "sect")),
    )
    return jax.shard_map(
        local,
        mesh=mesh,
        in_specs=placed,
        out_specs=(P(("dp", "sect"), "tensor"), P(("dp", "sect"), "tensor", None)),
        check_vma=False,
    )
```

```python
import jax
import jax.numpy as jnp
from jax import lax
from jax.sharding import PartitionSpec as P

EXPERTS = 128
CAP = 5


def route_slots(expert_ids, experts, capacity):
    row_count = expert_ids.shape[0]
    named = expert_ids[:, :, None] == jnp.arange(experts, dtype=jnp.int32)[None, None, :]
    member = jnp.sum(named.astype(jnp.float32), axis=1)
    rows = jnp.arange(row_count, dtype=jnp.int32)
    earlier = (rows[:, None] > rows[None, :]).astype(jnp.float32)
    slot = jnp.dot(earlier, member, preferred_element_type=jnp.float32)
    level = jnp.arange(capacity, dtype=jnp.float32)[None, :, None]
    hit = (slot.T[:, None, :] == level) & (member.T[:, None, :] > 0)
    dispatch = jnp.where(hit, 1.0, 0.0).reshape(experts * capacity, row_count)
    return dispatch.astype(jnp.bfloat16), hit


def route_combine(expert_ids, weights, hit, experts, capacity):
    row_count = expert_ids.shape[0]
    named = expert_ids[:, :, None] == jnp.arange(experts, dtype=jnp.int32)[None, None, :]
    share_norm = (weights / jnp.sum(weights, axis=1, keepdims=True)).astype(jnp.bfloat16)
    share_norm = lax.optimization_barrier(share_norm).astype(jnp.float32)
    share_of = jnp.sum(jnp.where(named, share_norm[:, :, None], 0.0), axis=1)
    combine = jnp.where(hit, share_of.T[:, None, :], 0.0).reshape(experts * capacity, row_count)
    return combine.astype(jnp.bfloat16)

def attend(query, cache_keys, cache_values, lengths):
    row_count, head_count, head_size = query.shape
    kv_count = cache_keys.shape[2]
    group_size = head_count // kv_count
    queries = query.reshape(row_count, kv_count, group_size, head_size)
    scores = jnp.einsum(
        "rkgd,rlkd->rkgl", queries, cache_keys, preferred_element_type=jnp.float32
    ) * head_size ** (-0.5)
    valid = jnp.arange(cache_keys.shape[1], dtype=jnp.int32)[None, :] < lengths[:, None]
    scores = jnp.where(valid[:, None, None, :], scores, -1e30)
    highest = jnp.max(scores, axis=3, keepdims=True)
    expo = jnp.exp(scores - highest)
    probs = (expo / jnp.sum(expo, axis=3, keepdims=True)).astype(jnp.bfloat16)
    result = jnp.einsum("rkgl,rlkd->rkgd", probs, cache_values, preferred_element_type=jnp.float32)
    return result.astype(jnp.bfloat16).reshape(row_count, head_count, head_size)


def shifted(x, step, count):
    return lax.ppermute(x, "tensor", perm=[(i, (i + step) % count) for i in range(count)])


def ring_projections(inputs, gate_weight, up_weight, count):
    width = inputs.shape[2]
    if count != 4:
        gathered = lax.all_gather(inputs, "tensor", axis=2, tiled=True)
        gate = jnp.einsum("end,edf->enf", gathered, gate_weight, preferred_element_type=jnp.float32)
        up = jnp.einsum("end,edf->enf", gathered, up_weight, preferred_element_type=jnp.float32)
        return gate, up
    me = lax.axis_index("tensor")
    from_left = shifted(inputs, 1, count)
    from_right = shifted(inputs, -1, count)
    far = shifted(from_right, -1, count)
    gate = None
    up = None
    for piece, offset in ((inputs, 0), (from_left, count - 1), (from_right, 1), (far, 2)):
        start = ((me + offset) % count) * width
        gate_rows = lax.dynamic_slice_in_dim(gate_weight, start, width, axis=1)
        up_rows = lax.dynamic_slice_in_dim(up_weight, start, width, axis=1)
        g = jnp.einsum("end,edf->enf", piece, gate_rows, preferred_element_type=jnp.float32)
        u = jnp.einsum("end,edf->enf", piece, up_rows, preferred_element_type=jnp.float32)
        gate = g if gate is None else gate + g
        up = u if up is None else up + u
    return gate, up


def split_down(down_weight, count):
    width = down_weight.shape[2] // count
    if count != 4:
        return lax.all_to_all(
            down_weight.reshape(down_weight.shape[0], down_weight.shape[1], count, width)
            .transpose(2, 0, 1, 3),
            "tensor",
            split_axis=0,
            concat_axis=0,
            tiled=True,
        )
    me = lax.axis_index("tensor")

    def columns(offset):
        start = ((me + offset) % count) * width
        return lax.dynamic_slice_in_dim(down_weight, start, width, axis=2)

    return (
        columns(0),
        shifted(columns(1), 1, count),
        shifted(columns(count - 1), -1, count),
        shifted(columns(2), 2, count),
    )


def down_projection(hidden_t, down_pieces, count):
    hidden_all = lax.all_gather(hidden_t, "tensor", axis=0, tiled=False)
    if count != 4:
        group_sums = jnp.einsum(
            "gefn,gefc->genc", hidden_all, down_pieces, preferred_element_type=jnp.float32
        ).astype(jnp.bfloat16)
        return jnp.sum(group_sums.astype(jnp.float32), axis=0).astype(jnp.bfloat16)
    me = lax.axis_index("tensor")
    total = None
    for offset, weight in zip((0, count - 1, 1, 2), down_pieces):
        piece = lax.dynamic_index_in_dim(hidden_all, (me + offset) % count, axis=0, keepdims=False)
        group = jnp.einsum("efn,efc->enc", piece, weight, preferred_element_type=jnp.float32)
        group = group.astype(jnp.bfloat16).astype(jnp.float32)
        total = group if total is None else total + group
    return total.astype(jnp.bfloat16)


def local(
    tokens,
    route_experts,
    route_weights,
    gate_weight,
    up_weight,
    down_weight,
    query,
    cache_keys,
    cache_values,
    lengths,
):
    owners = lax.axis_size("dp") * lax.axis_size("sect")
    dispatch, hit = route_slots(route_experts, EXPERTS, CAP)
    slot_total = EXPERTS * CAP
    per_owner = slot_total // owners
    local_buffer = jnp.dot(dispatch, tokens, preferred_element_type=jnp.float32).astype(
        jnp.bfloat16
    )
    width = local_buffer.shape[1]
    lanes = 128
    local_buffer = local_buffer.reshape(owners, per_owner * width // lanes, lanes)
    down_pieces = split_down(down_weight, lax.axis_size("tensor"))
    arrived = lax.all_to_all(local_buffer, ("dp", "sect"), split_axis=0, concat_axis=0, tiled=True)
    arrived, late_ids, late_weights, late_hit, down_pieces = lax.optimization_barrier(
        (arrived, route_experts, route_weights, hit, down_pieces)
    )
    combine = route_combine(late_ids, late_weights, late_hit, EXPERTS, CAP)
    own_experts = gate_weight.shape[0]
    pieces = lax.axis_size("tensor")
    inputs = (
        arrived.reshape(owners, own_experts, CAP, width)
        .transpose(1, 0, 2, 3)
        .reshape(own_experts, owners * CAP, width)
    )
    hidden_width = gate_weight.shape[2]
    gate_part, up_part = ring_projections(inputs, gate_weight, up_weight, pieces)
    hidden = (jax.nn.silu(gate_part) * up_part).astype(jnp.bfloat16)
    summed = down_projection(hidden.transpose(0, 2, 1), down_pieces, pieces)
    last = summed.shape[2]
    returned = lax.all_to_all(
        summed.reshape(own_experts, owners, CAP, last)
        .transpose(1, 0, 2, 3)
        .reshape(owners, own_experts * CAP * last // lanes, lanes),
        ("dp", "sect"),
        split_axis=0,
        concat_axis=0,
        tiled=True,
    )
    expert_out = returned.reshape(slot_total, last)
    mixture = jnp.dot(combine.T, expert_out, preferred_element_type=jnp.float32).astype(
        jnp.bfloat16
    )
    attention = attend(query, cache_keys, cache_values, lengths)
    return (mixture, attention)


def solution(mesh):
    placed = (
        P(("dp", "sect"), "tensor"),
        P(("dp", "sect"), None),
        P(("dp", "sect"), None),
        P(("dp", "sect"), None, "tensor"),
        P(("dp", "sect"), None, "tensor"),
        P(("dp", "sect"), "tensor", None),
        P(("dp", "sect"), "tensor", None),
        P(("dp", "sect"), None, "tensor", None),
        P(("dp", "sect"), None, "tensor", None),
        P(("dp", "sect")),
    )
    return jax.shard_map(
        local,
        mesh=mesh,
        in_specs=placed,
        out_specs=(P(("dp", "sect"), "tensor"), P(("dp", "sect"), "tensor", None)),
        check_vma=False,
    )
```

```python
import jax
import jax.numpy as jnp
from jax import lax
from jax.sharding import PartitionSpec as P

EXPERTS = 128
CAP = 5


def route_slots(expert_ids, experts, capacity):
    row_count = expert_ids.shape[0]
    named = expert_ids[:, :, None] == jnp.arange(experts, dtype=jnp.int32)[None, None, :]
    member = jnp.sum(named.astype(jnp.float32), axis=1)
    rows = jnp.arange(row_count, dtype=jnp.int32)
    earlier = (rows[:, None] > rows[None, :]).astype(jnp.float32)
    slot = jnp.dot(earlier, member, preferred_element_type=jnp.float32)
    level = jnp.arange(capacity, dtype=jnp.float32)[None, :, None]
    hit = (slot.T[:, None, :] == level) & (member.T[:, None, :] > 0)
    dispatch = jnp.where(hit, 1.0, 0.0).reshape(experts * capacity, row_count)
    return dispatch.astype(jnp.bfloat16), hit


def route_combine(expert_ids, weights, hit, experts, capacity):
    row_count = expert_ids.shape[0]
    named = expert_ids[:, :, None] == jnp.arange(experts, dtype=jnp.int32)[None, None, :]
    share_norm = (weights / jnp.sum(weights, axis=1, keepdims=True)).astype(jnp.bfloat16)
    share_norm = lax.optimization_barrier(share_norm).astype(jnp.float32)
    share_of = jnp.sum(jnp.where(named, share_norm[:, :, None], 0.0), axis=1)
    combine = jnp.where(hit, share_of.T[:, None, :], 0.0).reshape(experts * capacity, row_count)
    return combine.astype(jnp.bfloat16)

def attend(query, cache_keys, cache_values, lengths):
    row_count, head_count, head_size = query.shape
    kv_count = cache_keys.shape[2]
    group_size = head_count // kv_count
    queries = query.reshape(row_count, kv_count, group_size, head_size)
    scores = jnp.einsum(
        "rkgd,rlkd->rkgl", queries, cache_keys, preferred_element_type=jnp.float32
    ) * head_size ** (-0.5)
    valid = jnp.arange(cache_keys.shape[1], dtype=jnp.int32)[None, :] < lengths[:, None]
    scores = jnp.where(valid[:, None, None, :], scores, -1e30)
    highest = jnp.max(scores, axis=3, keepdims=True)
    expo = jnp.exp(scores - highest)
    probs = (expo / jnp.sum(expo, axis=3, keepdims=True)).astype(jnp.bfloat16)
    result = jnp.einsum("rkgl,rlkd->rkgd", probs, cache_values, preferred_element_type=jnp.float32)
    return result.astype(jnp.bfloat16).reshape(row_count, head_count, head_size)


def shifted(x, step, count):
    return lax.ppermute(x, "tensor", perm=[(i, (i + step) % count) for i in range(count)])


def ring_projections(inputs, gate_weight, up_weight, count):
    width = inputs.shape[2]
    if count != 4:
        gathered = lax.all_gather(inputs, "tensor", axis=2, tiled=True)
        gate = jnp.einsum("end,edf->enf", gathered, gate_weight, preferred_element_type=jnp.float32)
        up = jnp.einsum("end,edf->enf", gathered, up_weight, preferred_element_type=jnp.float32)
        return gate, up
    me = lax.axis_index("tensor")
    half = inputs.shape[1] // 2
    top, bottom = inputs[:, :half], inputs[:, half:]
    left_bottom = shifted(bottom, 1, count)
    from_right = shifted(inputs, -1, count)
    right_top = from_right[:, :half]
    from_left = jnp.concatenate([shifted(top, 1, count), left_bottom], axis=1)
    far = jnp.concatenate([shifted(right_top, -1, count), shifted(left_bottom, 1, count)], axis=1)
    gate = None
    up = None
    for piece, offset in ((inputs, 0), (from_left, count - 1), (from_right, 1), (far, 2)):
        start = ((me + offset) % count) * width
        gate_rows = lax.dynamic_slice_in_dim(gate_weight, start, width, axis=1)
        up_rows = lax.dynamic_slice_in_dim(up_weight, start, width, axis=1)
        g = jnp.einsum("end,edf->enf", piece, gate_rows, preferred_element_type=jnp.float32)
        u = jnp.einsum("end,edf->enf", piece, up_rows, preferred_element_type=jnp.float32)
        gate = g if gate is None else gate + g
        up = u if up is None else up + u
    return gate, up


def split_down(down_weight, count):
    width = down_weight.shape[2] // count
    if count != 4:
        return lax.all_to_all(
            down_weight.reshape(down_weight.shape[0], down_weight.shape[1], count, width)
            .transpose(2, 0, 1, 3),
            "tensor",
            split_axis=0,
            concat_axis=0,
            tiled=True,
        )
    me = lax.axis_index("tensor")

    def columns(offset):
        start = ((me + offset) % count) * width
        return lax.dynamic_slice_in_dim(down_weight, start, width, axis=2)

    return (
        columns(0),
        shifted(columns(1), 1, count),
        shifted(columns(count - 1), -1, count),
        shifted(columns(2), 2, count),
    )


def down_projection(hidden_t, down_pieces, count):
    hidden_all = lax.all_gather(hidden_t, "tensor", axis=0, tiled=False)
    if count != 4:
        group_sums = jnp.einsum(
            "gefn,gefc->genc", hidden_all, down_pieces, preferred_element_type=jnp.float32
        ).astype(jnp.bfloat16)
        return jnp.sum(group_sums.astype(jnp.float32), axis=0).astype(jnp.bfloat16)
    me = lax.axis_index("tensor")
    total = None
    for offset, weight in zip((0, count - 1, 1, 2), down_pieces):
        piece = lax.dynamic_index_in_dim(hidden_all, (me + offset) % count, axis=0, keepdims=False)
        group = jnp.einsum("efn,efc->enc", piece, weight, preferred_element_type=jnp.float32)
        group = group.astype(jnp.bfloat16).astype(jnp.float32)
        total = group if total is None else total + group
    return total.astype(jnp.bfloat16)


def local(
    tokens,
    route_experts,
    route_weights,
    gate_weight,
    up_weight,
    down_weight,
    query,
    cache_keys,
    cache_values,
    lengths,
):
    owners = lax.axis_size("dp") * lax.axis_size("sect")
    dispatch, hit = route_slots(route_experts, EXPERTS, CAP)
    slot_total = EXPERTS * CAP
    per_owner = slot_total // owners
    local_buffer = jnp.dot(dispatch, tokens, preferred_element_type=jnp.float32).astype(
        jnp.bfloat16
    )
    width = local_buffer.shape[1]
    lanes = 128
    local_buffer = local_buffer.reshape(owners, per_owner * width // lanes, lanes)
    down_pieces = split_down(down_weight, lax.axis_size("tensor"))
    arrived = lax.all_to_all(local_buffer, ("dp", "sect"), split_axis=0, concat_axis=0, tiled=True)
    arrived, late_ids, late_weights, late_hit, down_pieces = lax.optimization_barrier(
        (arrived, route_experts, route_weights, hit, down_pieces)
    )
    combine = route_combine(late_ids, late_weights, late_hit, EXPERTS, CAP)
    own_experts = gate_weight.shape[0]
    pieces = lax.axis_size("tensor")
    inputs = (
        arrived.reshape(owners, own_experts, CAP, width)
        .transpose(1, 0, 2, 3)
        .reshape(own_experts, owners * CAP, width)
    )
    hidden_width = gate_weight.shape[2]
    gate_part, up_part = ring_projections(inputs, gate_weight, up_weight, pieces)
    hidden = (jax.nn.silu(gate_part) * up_part).astype(jnp.bfloat16)
    summed = down_projection(hidden.transpose(0, 2, 1), down_pieces, pieces)
    last = summed.shape[2]
    returned = lax.all_to_all(
        summed.reshape(own_experts, owners, CAP, last)
        .transpose(1, 0, 2, 3)
        .reshape(owners, own_experts * CAP * last // lanes, lanes),
        ("dp", "sect"),
        split_axis=0,
        concat_axis=0,
        tiled=True,
    )
    expert_out = returned.reshape(slot_total, last)
    mixture = jnp.dot(combine.T, expert_out, preferred_element_type=jnp.float32).astype(
        jnp.bfloat16
    )
    attention = attend(query, cache_keys, cache_values, lengths)
    return (mixture, attention)


def solution(mesh):
    placed = (
        P(("dp", "sect"), "tensor"),
        P(("dp", "sect"), None),
        P(("dp", "sect"), None),
        P(("dp", "sect"), None, "tensor"),
        P(("dp", "sect"), None, "tensor"),
        P(("dp", "sect"), "tensor", None),
        P(("dp", "sect"), "tensor", None),
        P(("dp", "sect"), None, "tensor", None),
        P(("dp", "sect"), None, "tensor", None),
        P(("dp", "sect")),
    )
    return jax.shard_map(
        local,
        mesh=mesh,
        in_specs=placed,
        out_specs=(P(("dp", "sect"), "tensor"), P(("dp", "sect"), "tensor", None)),
        check_vma=False,
    )
```
